256 devices in a mesh: dp: 8 (over x, core), expert: 32 (over z, y).
Axes of the slice: x: 4, y: 4, z: 8, core: 2. Of those that a mesh axis runs over, the one named last changes fastest.
Arguments:
- tokens: bfloat16 [32768, 2048], P(('dp', 'expert')), may hold values from -6 to 6
- cotangent: bfloat16 [32768, 2048], P(('dp', 'expert')), may hold values from -0.875 to 0.875
- expert_ids: int32 [32768, 8], P(('dp', 'expert')), may hold values from 0 to 31, all different within a row; in each aligned block of 128 rows (0 to 127, 128 to 255, ...) at most 36 rows name the same one
- combine: float32 [32768, 8], P(('dp', 'expert')), may hold values from 0.02 to 0.5
- w_gate: bfloat16 [32, 2048, 512], P('expert'), may hold values from -0.125 to 0.125
- w_up: bfloat16 [32, 2048, 512], P('expert'), may hold values from -0.125 to 0.125
- w_down: bfloat16 [32, 512, 2048], P('expert'), may hold values from -0.25 to 0.25
- tangent_gate: bfloat16 [32, 2048, 512], P('expert'), may hold values from -0.125 to 0.125
Outputs:
- hvp_gate: float32 [32, 2048, 512], P('expert', 'dp')
- output_tangent: bfloat16 [32768, 2048], P(('dp', 'expert'))
The draws below stay inside these ranges and needn't reach their ends.
Inputs may be any that keep to these rules, and one draw needn't show every extreme that they name: `expert_ids`: A row names 8 different experts; among the 128 rows of one device no expert is named by more than 36 rows, and in every draw some expert is named by exactly 36 rows of some device.
All inputs are finite; a program needn't handle non-finite values.
Results may differ from the reference program's by a relative error of at most 0.0057.
Values may be sent and summed in bfloat16 or wider, within the bound.
No kernel may reach another device: no remote copies, remote signals or barrier semaphores. Data moves between devices by JAX's collectives and lax.ppermute only.
A program may use at most 128 MiB of HBM per device.

```python
import math
import jax
import jax.numpy as jnp
import numpy as np
from jax import lax

D = 2048
FF = 512
TOPK = 8
TOK_DEV = 128
EXPERTS = 32
CAP = 36
TOKENS = 32768
N_DP = 8
N_EXPERT = 32


def steps_of(stream_key, shape, cuts, least, largest):
    def one(position, blocks):
        heights = jax.random.uniform(jax.random.fold_in(jax.random.fold_in(stream_key, 6), position), (blocks,), jnp.float32, least / len(cuts), largest / len(cuts))
        return jnp.repeat(jnp.exp(heights), shape[position] // blocks).reshape((-1,) + (1,) * (len(shape) - position - 1))

    level = one(*cuts[0])
    for cut in cuts[1:]:
        level = level * one(*cut)
    return level


def shared_out(key, own, number, rows, count, top, reach, slope):
    order = jax.random.permutation(key, count)
    packed, common = portions_of(count, rows * top, reach, slope, True), portions_of(count, rows * top, reach, slope, False)
    places = jnp.arange(count)

    def named(lengths, offset_by):
        used = int((lengths > 0).sum())
        fixed = max(1, used // 4)
        shifted = fixed + (places - fixed + offset_by * (used - fixed)) % max(1, count - fixed)
        return jnp.zeros((count,), jnp.int32).at[order[jnp.where(places < fixed, places, shifted)]].set(jnp.asarray(lengths, jnp.int32))

    lengths = jnp.where(number % 4 == 0, named(packed, number // 4), named(common, number - number // 4 - 1))
    mixed = jax.random.permutation(jax.random.fold_in(own, 3), count)
    source_of, receiver = mixed[0:count // 2 * 2:2], mixed[1:count // 2 * 2:2]
    slack = jnp.minimum(lengths[source_of] - 1, reach - lengths[receiver]) // 2
    slack = jnp.where((source_of == order[0]) | (receiver == order[0]) | (lengths[receiver] == 0), 0, jnp.maximum(slack, 0))
    shifted = jax.random.randint(jax.random.fold_in(own, 4), (count // 2,), 0, 1 << 20) % (slack + 1)
    lengths = lengths.at[source_of].add(-shifted).at[receiver].add(shifted)
    members = jnp.searchsorted(jnp.cumsum(lengths), jnp.arange(rows * top), side="right").astype(jnp.int32)
    grid = members.reshape(top, rows).T
    grid = grid[jax.random.permutation(jax.random.fold_in(own, 1), rows)]
    offset_by = jax.random.randint(jax.random.fold_in(own, 2), (rows, 1), 0, top)
    return jnp.take_along_axis(grid, (jnp.arange(top)[None, :] + offset_by) % top, axis=1)


def portions_of(number_of, total, limit, lean, full):
    weights = [(1 << 20) // math.isqrt(standing ** lean) + 1 for standing in range(1, number_of + 1)]
    largest = limit if full else min(limit, max(-(-total // number_of), total * weights[0] // sum(weights)))
    least = 1 if total - largest >= number_of - 1 else 0
    holding, spare = [largest] + [least] * (number_of - 1), total - largest - least * (number_of - 1)
    while spare > 0:
        free = [i for i in range(1, number_of) if holding[i] < largest] or [i for i in range(1, number_of) if holding[i] < limit]
        whole, remaining = sum([weights[i] for i in free]), spare
        for i in free:
            addition = min(limit - holding[i], max(1, remaining * weights[i] // whole), spare)
            holding[i] = holding[i] + addition
            spare = spare - addition
    return np.array(holding)


def noise(stream_key, dims, deviation, reach, shards=(), held_as=jnp.bfloat16):
    drawn = jax.random.normal(stream_key, dims, jnp.float32) * deviation
    if len(shards) > 0:
        drawn = steps_of(stream_key, dims, shards, -0.22, 0.18) * drawn
    return jnp.clip(drawn, min=-reach, max=reach).astype(held_as)


def setup_inputs(seed: int = 0) -> dict:
    key_of = jax.random.split(jax.random.key(seed), 9)
    tokens = noise(key_of[0], (TOKENS, D), 1.0, 6.0, ((0, 256),))
    cotangent = noise(key_of[1], (TOKENS, D), 0.15, 0.875, ((0, 256),))
    expert_ids_keys = jax.random.split(jax.random.fold_in(key_of[2], 1), TOKENS // TOK_DEV)
    expert_ids_turns = jax.random.permutation(jax.random.fold_in(key_of[2], 3), TOKENS // TOK_DEV)
    expert_ids = jax.vmap(lambda own, number: shared_out(jax.random.fold_in(key_of[2], 2), own, number, TOK_DEV, EXPERTS, TOPK, CAP, 1))(expert_ids_keys, expert_ids_turns).reshape((TOKENS, TOPK))
    combine = jnp.clip(jnp.exp(math.log(0.5) - 3.218876 * jax.random.uniform(key_of[3], (TOKENS, TOPK), jnp.float32) ** steps_of(key_of[3], (TOKENS, TOPK), ((0, 256),), -0.2, 0.2)), 0.02, 0.5)
    w_gate = noise(key_of[4], (EXPERTS, D, FF), D ** -0.5, 0.125, ((0, 32),))
    w_up = noise(key_of[5], (EXPERTS, D, FF), D ** -0.5, 0.125, ((0, 32),))
    w_down = noise(key_of[6], (EXPERTS, FF, D), FF ** -0.5, 0.25, ((0, 32),))
    tangent_gate = noise(key_of[7], (EXPERTS, D, FF), D ** -0.5, 0.125, ((0, 32),))
    return {"tokens": tokens, "cotangent": cotangent, "expert_ids": expert_ids, "combine": combine, "w_gate": w_gate, "w_up": w_up, "w_down": w_down, "tangent_gate": tangent_gate}


def silu_derivs(gate_act):
    squash = jax.nn.sigmoid(gate_act)
    first = squash * (1.0 + gate_act * (1.0 - squash))
    second = squash * (1.0 - squash) * (2.0 + gate_act * (1.0 - 2.0 * squash))
    return first, second


def expert_rows(rows, scaled, gate_e, up_e, down_e, tangent_e):
    gate_act = jnp.dot(rows, gate_e, preferred_element_type=jnp.float32)
    up_act = jnp.dot(rows, up_e, preferred_element_type=jnp.float32)
    gate_dot = jnp.dot(rows, tangent_e, preferred_element_type=jnp.float32)
    first, second = silu_derivs(gate_act)
    lifted = (first * gate_dot * up_act).astype(jnp.bfloat16)
    term = jnp.dot(lifted, down_e, preferred_element_type=jnp.float32).astype(jnp.bfloat16)
    factor = up_act * second * gate_dot
    back_hidden = lax.dot_general(scaled, down_e, (((1,), (1,)), ((), ())), preferred_element_type=jnp.float32)
    coeff = (back_hidden * factor).astype(jnp.bfloat16)
    partial_hvp = lax.dot_general(rows, coeff, (((0,), (0,)), ((), ())), preferred_element_type=jnp.float32)
    return term, partial_hvp


def reference(tokens, cotangent, expert_ids, combine, w_gate, w_up, w_down, tangent_gate):
    max_rows = N_DP * N_EXPERT * CAP
    token_count = tokens.shape[0]

    def visit(accumulate, stacked):
        expert_index, gate_e, up_e, down_e, tangent_e = stacked
        chosen = expert_ids == expert_index
        present = jnp.any(chosen, axis=1)
        weight_all = jnp.sum(jnp.where(chosen, combine, jnp.zeros_like(combine)), axis=1)
        row_index = jnp.nonzero(present, size=max_rows, fill_value=0)[0].astype(jnp.int32)
        valid = jnp.arange(max_rows, dtype=jnp.int32) < jnp.sum(present.astype(jnp.int32))
        picked_weight = weight_all[row_index]
        row_weight = jnp.where(valid, picked_weight, jnp.zeros_like(picked_weight))
        rows = tokens[row_index]
        scaled = (row_weight[:, None] * cotangent[row_index].astype(jnp.float32)).astype(jnp.bfloat16)
        term, partial_hvp = expert_rows(rows, scaled, gate_e, up_e, down_e, tangent_e)
        accumulate = accumulate.at[row_index].add(row_weight[:, None] * term.astype(jnp.float32))
        return accumulate, partial_hvp

    start_value = jnp.zeros((token_count, tokens.shape[1]), jnp.float32)
    numbers = jnp.arange(EXPERTS, dtype=jnp.int32)
    final, hvp_gate = lax.scan(visit, start_value, (numbers, w_gate, w_up, w_down, tangent_gate))
    return hvp_gate, final.astype(jnp.bfloat16)
```

```python
import jax
import jax.numpy as jnp
import numpy as np
from jax import lax
from jax.sharding import Mesh
from jax.sharding import PartitionSpec as P


def silu_derivs(gate_act):
    squash = jax.nn.sigmoid(gate_act)
    first = squash * (1.0 + gate_act * (1.0 - squash))
    second = squash * (1.0 - squash) * (2.0 + gate_act * (1.0 - 2.0 * squash))
    return (first, second)


def forward_part(rows_flat, gate_e, up_e, down_e, tangent_e):
    gate_act = jnp.dot(rows_flat, gate_e, preferred_element_type=jnp.float32)
    up_act = jnp.dot(rows_flat, up_e, preferred_element_type=jnp.float32)
    gate_dot = jnp.dot(rows_flat, tangent_e, preferred_element_type=jnp.float32)
    first, second = silu_derivs(gate_act)
    lifted = (first * gate_dot * up_act).astype(jnp.bfloat16)
    term = jnp.dot(lifted, down_e, preferred_element_type=jnp.float32).astype(jnp.bfloat16)
    return (term, up_act * second * gate_dot)


def backward_part(scaled_flat, down_e, factor):
    back_hidden = lax.dot_general(
        scaled_flat, down_e, (((1,), (1,)), ((), ())), preferred_element_type=jnp.float32
    )
    return (back_hidden * factor).astype(jnp.bfloat16)


def per_device(tokens, cotangent, expert_ids, combine, w_gate, w_up, w_down, tangent_gate):
    n_z = lax.axis_size("ez")
    n_y = lax.axis_size("ey")
    expert_count = n_z * n_y
    rows_dev, top_count = expert_ids.shape
    model_width = tokens.shape[1]
    capacity = rows_dev * top_count * 9 // (8 * expert_count)
    owners = jnp.arange(expert_count, dtype=jnp.int32)
    matches = (expert_ids[:, :, None] == owners[None, None, :]).astype(jnp.int32)
    named_count = jnp.sum(matches, axis=1)
    before = jnp.cumsum(named_count, axis=0) - named_count
    slot_pos = jnp.sum(before[:, None, :] * matches, axis=2)
    target = (expert_ids * capacity + slot_pos).reshape(-1)
    token_index = jnp.repeat(jnp.arange(rows_dev, dtype=jnp.float32), top_count)
    slots = expert_count * capacity
    table = jnp.stack(
        [
            jnp.full((slots,), -1.0, jnp.float32).at[target].set(token_index),
            jnp.zeros((slots,), jnp.float32).at[target].set(combine.reshape(-1)),
        ]
    ).reshape(2, expert_count, capacity)

    tok_g = lax.all_gather(tokens, "ez", axis=0, tiled=True)
    cot_g = lax.all_gather(cotangent, "ez", axis=0, tiled=True)
    table_g = lax.all_gather(table, "ez", axis=0)
    z_me = lax.axis_index("ez")
    mine = lax.dynamic_slice_in_dim(table_g, z_me * n_y, n_y, axis=2)
    mine = jnp.transpose(mine, (1, 2, 0, 3))
    src_tok, src_w = mine[0], mine[1]
    valid = src_tok >= 0.0
    gidx = jnp.where(
        valid,
        src_tok.astype(jnp.int32) + (jnp.arange(n_z, dtype=jnp.int32) * rows_dev)[None, :, None],
        0,
    ).reshape(-1)
    valid_flat = valid.reshape(-1)
    send_rows = jnp.where(valid_flat[:, None], tok_g[gidx], jnp.zeros((), tok_g.dtype))
    send_scaled = (src_w.reshape(-1)[:, None] * cot_g[gidx].astype(jnp.float32)).astype(jnp.bfloat16)

    def along_y(block):
        block = block.reshape(n_y, n_z, 1, capacity, model_width)
        got = lax.all_to_all(block, "ey", split_axis=0, concat_axis=2, tiled=True)
        return got.reshape(-1, model_width)

    rows_flat = along_y(send_rows)
    scaled_flat = along_y(send_scaled)
    gate_e = w_gate[0]
    up_e = w_up[0]
    down_e = w_down[0]
    tangent_e = tangent_gate[0]
    term, factor = forward_part(rows_flat, gate_e, up_e, down_e, tangent_e)
    returned = lax.all_to_all(
        term.reshape(expert_count, capacity, model_width),
        ("ez", "ey"),
        split_axis=0,
        concat_axis=0,
        tiled=True,
    )
    coeff = backward_part(scaled_flat, down_e, factor)
    partial_hvp = lax.dot_general(
        rows_flat, coeff, (((0,), (0,)), ((), ())), preferred_element_type=jnp.float32
    )
    hvp_gate = lax.psum_scatter(partial_hvp, "dp", scatter_dimension=0, tiled=True)
    returned_flat = returned.reshape(-1, model_width)
    picked = returned_flat[target].reshape(rows_dev, top_count, model_width)
    output_tangent = jnp.sum(combine[:, :, None] * picked.astype(jnp.float32), axis=1).astype(
        jnp.bfloat16
    )
    return (hvp_gate[None], output_tangent)


def y_size(mesh):
    column = mesh.devices[0]
    try:
        return len({int(d.coords[1]) for d in column})
    except Exception:
        return 4


def solution(mesh):
    n_dp, n_expert = mesh.devices.shape
    n_y = y_size(mesh)
    mesh3 = Mesh(mesh.devices.reshape(n_dp, n_expert // n_y, n_y), ("dp", "ez", "ey"))
    rows = P(("dp", "ez", "ey"), None)
    weights = P(("ez", "ey"), None, None)
    placed = (rows, rows, rows, rows, weights, weights, weights, weights)
    return jax.shard_map(
        per_device,
        mesh=mesh3,
        in_specs=placed,
        out_specs=(P(("ez", "ey"), "dp", None), rows),
        check_vma=False,
    )
```

```python
import jax
import jax.numpy as jnp
import numpy as np
from jax import lax
from jax.sharding import Mesh
from jax.sharding import PartitionSpec as P


def silu_derivs(gate_act):
    squash = jax.nn.sigmoid(gate_act)
    first = squash * (1.0 + gate_act * (1.0 - squash))
    second = squash * (1.0 - squash) * (2.0 + gate_act * (1.0 - 2.0 * squash))
    return (first, second)


def forward_part(rows_flat, gate_e, up_e, down_e, tangent_e):
    gate_act = jnp.dot(rows_flat, gate_e, preferred_element_type=jnp.float32)
    up_act = jnp.dot(rows_flat, up_e, preferred_element_type=jnp.float32)
    gate_dot = jnp.dot(rows_flat, tangent_e, preferred_element_type=jnp.float32)
    first, second = silu_derivs(gate_act)
    lifted = (first * gate_dot * up_act).astype(jnp.bfloat16)
    term = jnp.dot(lifted, down_e, preferred_element_type=jnp.float32).astype(jnp.bfloat16)
    return (term, up_act * second * gate_dot)


def backward_part(scaled_flat, down_e, factor):
    back_hidden = lax.dot_general(
        scaled_flat, down_e, (((1,), (1,)), ((), ())), preferred_element_type=jnp.float32
    )
    return (back_hidden * factor).astype(jnp.bfloat16)


def per_device(tokens, cotangent, expert_ids, combine, w_gate, w_up, w_down, tangent_gate):
    n_z = lax.axis_size("ez")
    n_y = lax.axis_size("ey")
    expert_count = n_z * n_y
    rows_dev, top_count = expert_ids.shape
    model_width = tokens.shape[1]
    capacity = rows_dev * top_count * 9 // (8 * expert_count)
    owners = jnp.arange(expert_count, dtype=jnp.int32)
    matches = (expert_ids[:, :, None] == owners[None, None, :]).astype(jnp.int32)
    named_count = jnp.sum(matches, axis=1)
    before = jnp.cumsum(named_count, axis=0) - named_count
    slot_pos = jnp.sum(before[:, None, :] * matches, axis=2)
    target = (expert_ids * capacity + slot_pos).reshape(-1)
    slots = expert_count * capacity
    token_index = jnp.repeat(jnp.arange(rows_dev, dtype=jnp.float32), top_count)
    src_of = jnp.full((slots,), -1.0, jnp.float32).at[target].set(token_index)
    w_of = jnp.zeros((slots,), jnp.float32).at[target].set(combine.reshape(-1))
    w_hi = lax.reduce_precision(w_of, exponent_bits=8, mantissa_bits=7)
    rest = w_of - w_hi
    w_mid = lax.reduce_precision(rest, exponent_bits=8, mantissa_bits=7)
    w_lo = rest - w_mid
    table = jnp.stack([src_of, w_hi, w_mid, w_lo]).astype(jnp.bfloat16)
    extra = 16
    table = jnp.pad(table.reshape(-1), (0, extra * model_width - 4 * slots))
    packed = jnp.concatenate([tokens, table.reshape(extra, model_width)], axis=0)

    tok_g = lax.all_gather(packed, "ez", axis=0)
    cot_g = lax.all_gather(cotangent, "ez", axis=0, tiled=True)
    table_g = tok_g[:, rows_dev:].reshape(n_z, -1)[:, : 4 * slots].reshape(n_z, 4, expert_count, capacity)
    tok_g = tok_g[:, :rows_dev].reshape(n_z * rows_dev, model_width)
    z_me = lax.axis_index("ez")
    mine = lax.dynamic_slice_in_dim(table_g, z_me * n_y, n_y, axis=2).astype(jnp.float32)
    mine = jnp.transpose(mine, (1, 2, 0, 3))
    src_tok = mine[0]
    src_w = (mine[1] + mine[2]) + mine[3]
    gidx = jnp.maximum(
        src_tok.astype(jnp.int32) + (jnp.arange(n_z, dtype=jnp.int32) * rows_dev)[None, :, None], 0
    ).reshape(-1)
    send_rows = tok_g[gidx]
    send_scaled = (src_w.reshape(-1)[:, None] * cot_g[gidx].astype(jnp.float32)).astype(jnp.bfloat16)

    rows_flat = lax.all_to_all(send_rows, "ey", split_axis=0, concat_axis=0, tiled=True)
    scaled_flat = lax.all_to_all(send_scaled, "ey", split_axis=0, concat_axis=0, tiled=True)
    gate_e = w_gate[0]
    up_e = w_up[0]
    down_e = w_down[0]
    tangent_e = tangent_gate[0]
    term, factor = forward_part(rows_flat, gate_e, up_e, down_e, tangent_e)
    returned = lax.all_to_all(term, ("ey", "ez"), split_axis=0, concat_axis=0, tiled=True)
    coeff = backward_part(scaled_flat, down_e, factor)
    partial_hvp = lax.dot_general(
        rows_flat, coeff, (((0,), (0,)), ((), ())), preferred_element_type=jnp.float32
    )
    hvp_gate = lax.psum_scatter(partial_hvp, "dp", scatter_dimension=0, tiled=True)
    back_at = (((expert_ids % n_y) * n_z + expert_ids // n_y) * capacity + slot_pos).reshape(-1)
    picked = returned[back_at].reshape(rows_dev, top_count, model_width)
    output_tangent = jnp.sum(combine[:, :, None] * picked.astype(jnp.float32), axis=1).astype(
        jnp.bfloat16
    )
    return (hvp_gate[None], output_tangent)


def y_size(mesh):
    column = mesh.devices[0]
    try:
        return len({int(d.coords[1]) for d in column})
    except Exception:
        return 4


def solution(mesh):
    n_dp, n_expert = mesh.devices.shape
    n_y = y_size(mesh)
    mesh3 = Mesh(mesh.devices.reshape(n_dp, n_expert // n_y, n_y), ("dp", "ez", "ey"))
    rows = P(("dp", "ez", "ey"), None)
    weights = P(("ez", "ey"), None, None)
    placed = (rows, rows, rows, rows, weights, weights, weights, weights)
    return jax.shard_map(
        per_device,
        mesh=mesh3,
        in_specs=placed,
        out_specs=(P(("ez", "ey"), "dp", None), rows),
        check_vma=False,
    )
```

```python
import jax
import jax.numpy as jnp
import numpy as np
from jax import lax
from jax.sharding import Mesh
from jax.sharding import PartitionSpec as P


def silu_derivs(gate_act):
    squash = jax.nn.sigmoid(gate_act)
    first = squash * (1.0 + gate_act * (1.0 - squash))
    second = squash * (1.0 - squash) * (2.0 + gate_act * (1.0 - 2.0 * squash))
    return (first, second)


def forward_part(rows_flat, gate_e, up_e, down_e, tangent_e):
    gate_act = jnp.dot(rows_flat, gate_e, preferred_element_type=jnp.float32)
    up_act = jnp.dot(rows_flat, up_e, preferred_element_type=jnp.float32)
    gate_dot = jnp.dot(rows_flat, tangent_e, preferred_element_type=jnp.float32)
    first, second = silu_derivs(gate_act)
    lifted = (first * gate_dot * up_act).astype(jnp.bfloat16)
    term = jnp.dot(lifted, down_e, preferred_element_type=jnp.float32).astype(jnp.bfloat16)
    return (term, up_act * second * gate_dot)


def backward_part(scaled_flat, down_e, factor):
    back_hidden = lax.dot_general(
        scaled_flat, down_e, (((1,), (1,)), ((), ())), preferred_element_type=jnp.float32
    )
    return (back_hidden * factor).astype(jnp.bfloat16)


def split3(value):
    hi = lax.reduce_precision(value, exponent_bits=8, mantissa_bits=7)
    rest = value - hi
    mid = lax.reduce_precision(rest, exponent_bits=8, mantissa_bits=7)
    return (hi, mid, rest - mid)


def select_rows(index, source):
    picks = (index[:, None] == jnp.arange(source.shape[0], dtype=jnp.int32)[None, :]).astype(source.dtype)
    return jnp.dot(picks, source, preferred_element_type=jnp.float32)


def per_device(tokens, cotangent, expert_ids, combine, w_gate, w_up, w_down, tangent_gate):
    n_z = lax.axis_size("ez")
    n_y = lax.axis_size("ey")
    expert_count = n_z * n_y
    rows_dev, top_count = expert_ids.shape
    model_width = tokens.shape[1]
    capacity = rows_dev * top_count * 9 // (8 * expert_count)
    owners = jnp.arange(expert_count, dtype=jnp.int32)
    chosen = expert_ids[:, :, None] == owners[None, None, :]
    matches = chosen.astype(jnp.int32)
    named_count = jnp.sum(matches, axis=1)
    before = jnp.cumsum(named_count, axis=0) - named_count
    slot_pos = jnp.sum(before[:, None, :] * matches, axis=2)
    slots = expert_count * capacity
    in_slot = (named_count[:, :, None] > 0) & (
        before[:, :, None] == jnp.arange(capacity, dtype=jnp.int32)[None, None, :]
    )
    token_no = jnp.arange(rows_dev, dtype=jnp.float32)[:, None, None]
    src_of = jnp.sum(jnp.where(in_slot, token_no + 1.0, 0.0), axis=0) - 1.0
    weight_te = jnp.sum(jnp.where(chosen, combine[:, :, None], 0.0), axis=1)
    w_of = jnp.sum(jnp.where(in_slot, weight_te[:, :, None], 0.0), axis=0)
    table = jnp.stack((src_of,) + split3(w_of)).astype(jnp.bfloat16)
    extra = 16
    table = jnp.pad(table.reshape(-1), (0, extra * model_width - 4 * slots))
    packed = jnp.concatenate([tokens, table.reshape(extra, model_width)], axis=0)
    block = rows_dev + extra

    tok_g = lax.all_gather(packed, "ez", axis=0, tiled=True)
    cot_g = lax.all_gather(cotangent, "ez", axis=0, tiled=True)
    table_g = tok_g.reshape(n_z, block, model_width)[:, rows_dev:].reshape(n_z, -1)
    table_g = table_g[:, : 4 * slots].reshape(n_z, 4, expert_count, capacity)
    z_me = lax.axis_index("ez")
    mine = lax.dynamic_slice_in_dim(table_g, z_me * n_y, n_y, axis=2).astype(jnp.float32)
    mine = jnp.transpose(mine, (1, 2, 0, 3))
    src_tok = mine[0].astype(jnp.int32)
    src_w = (mine[1] + mine[2]) + mine[3]
    valid = src_tok >= 0
    z_of = jnp.arange(n_z, dtype=jnp.int32)[None, :, None]
    at_packed = jnp.where(valid, src_tok + z_of * block, -1).reshape(-1)
    at_cot = jnp.where(valid, src_tok + z_of * rows_dev, -1).reshape(-1)
    send_rows = select_rows(at_packed, tok_g).astype(jnp.bfloat16)
    send_scaled = (src_w.reshape(-1)[:, None] * select_rows(at_cot, cot_g)).astype(jnp.bfloat16)

    rows_flat = lax.all_to_all(send_rows, "ey", split_axis=0, concat_axis=0, tiled=True)
    scaled_flat = lax.all_to_all(send_scaled, "ey", split_axis=0, concat_axis=0, tiled=True)
    gate_e = w_gate[0]
    up_e = w_up[0]
    down_e = w_down[0]
    tangent_e = tangent_gate[0]
    term, factor = forward_part(rows_flat, gate_e, up_e, down_e, tangent_e)
    returned = lax.all_to_all(term, ("ey", "ez"), split_axis=0, concat_axis=0, tiled=True)
    coeff = backward_part(scaled_flat, down_e, factor)
    partial_hvp = lax.dot_general(
        rows_flat, coeff, (((0,), (0,)), ((), ())), preferred_element_type=jnp.float32
    )
    hvp_gate = lax.psum_scatter(partial_hvp, "dp", scatter_dimension=0, tiled=True)
    back_at = ((expert_ids % n_y) * n_z + expert_ids // n_y) * capacity + slot_pos
    at_slot = back_at[:, :, None] == jnp.arange(slots, dtype=jnp.int32)[None, None, :]
    output_tangent = jnp.zeros((rows_dev, model_width), jnp.float32)
    for piece in split3(combine):
        spread = jnp.sum(jnp.where(at_slot, piece[:, :, None], 0.0), axis=1).astype(jnp.bfloat16)
        output_tangent = output_tangent + jnp.dot(spread, returned, preferred_element_type=jnp.float32)
    return (hvp_gate[None], output_tangent.astype(jnp.bfloat16))


def y_size(mesh):
    column = mesh.devices[0]
    try:
        return len({int(d.coords[1]) for d in column})
    except Exception:
        return 4


def solution(mesh):
    n_dp, n_expert = mesh.devices.shape
    n_y = y_size(mesh)
    mesh3 = Mesh(mesh.devices.reshape(n_dp, n_expert // n_y, n_y), ("dp", "ez", "ey"))
    rows = P(("dp", "ez", "ey"), None)
    weights = P(("ez", "ey"), None, None)
    placed = (rows, rows, rows, rows, weights, weights, weights, weights)
    return jax.shard_map(
        per_device,
        mesh=mesh3,
        in_specs=placed,
        out_specs=(P(("ez", "ey"), "dp", None), rows),
        check_vma=False,
    )
```

```python
import jax
import jax.numpy as jnp
import numpy as np
from jax import lax
from jax.sharding import Mesh
from jax.sharding import PartitionSpec as P


def silu_derivs(gate_act):
    squash = jax.nn.sigmoid(gate_act)
    first = squash * (1.0 + gate_act * (1.0 - squash))
    second = squash * (1.0 - squash) * (2.0 + gate_act * (1.0 - 2.0 * squash))
    return (first, second)


def forward_part(rows_flat, gate_e, up_e, down_e, tangent_e):
    gate_act = jnp.dot(rows_flat, gate_e, preferred_element_type=jnp.float32)
    up_act = jnp.dot(rows_flat, up_e, preferred_element_type=jnp.float32)
    gate_dot = jnp.dot(rows_flat, tangent_e, preferred_element_type=jnp.float32)
    first, second = silu_derivs(gate_act)
    lifted = (first * gate_dot * up_act).astype(jnp.bfloat16)
    term = jnp.dot(lifted, down_e, preferred_element_type=jnp.float32).astype(jnp.bfloat16)
    return (term, up_act * second * gate_dot)


def backward_part(scaled_flat, down_e, factor):
    back_hidden = lax.dot_general(
        scaled_flat, down_e, (((1,), (1,)), ((), ())), preferred_element_type=jnp.float32
    )
    return (back_hidden * factor).astype(jnp.bfloat16)


def split3(value):
    hi = lax.reduce_precision(value, exponent_bits=8, mantissa_bits=7)
    rest = value - hi
    mid = lax.reduce_precision(rest, exponent_bits=8, mantissa_bits=7)
    return (hi, mid, rest - mid)


def select_rows(index, source):
    picks = (index[:, None] == jnp.arange(source.shape[0], dtype=jnp.int32)[None, :]).astype(source.dtype)
    return jnp.dot(picks, source, preferred_element_type=jnp.float32)


def shift_along_y(send, n_y):
    chunks = send.reshape(n_y, -1, send.shape[-1])
    me = lax.axis_index("ey")
    got = jnp.zeros_like(chunks)
    got = lax.dynamic_update_index_in_dim(got, lax.dynamic_index_in_dim(chunks, me, 0, False), me, 0)
    for shift in range(1, n_y):
        out = lax.dynamic_index_in_dim(chunks, (me + shift) % n_y, 0, False)
        moved = lax.ppermute(out, "ey", perm=[(i, (i + shift) % n_y) for i in range(n_y)])
        got = lax.dynamic_update_index_in_dim(got, moved, (me + n_y - shift) % n_y, 0)
    return got.reshape(send.shape)


def per_device(tokens, cotangent, expert_ids, combine, w_gate, w_up, w_down, tangent_gate):
    n_z = lax.axis_size("ez")
    n_y = lax.axis_size("ey")
    expert_count = n_z * n_y
    rows_dev, top_count = expert_ids.shape
    model_width = tokens.shape[1]
    capacity = rows_dev * top_count * 9 // (8 * expert_count)
    owners = jnp.arange(expert_count, dtype=jnp.int32)
    chosen = expert_ids[:, :, None] == owners[None, None, :]
    matches = chosen.astype(jnp.int32)
    named_count = jnp.sum(matches, axis=1)
    before = jnp.cumsum(named_count, axis=0) - named_count
    slot_pos = jnp.sum(before[:, None, :] * matches, axis=2)
    slots = expert_count * capacity
    in_slot = (named_count[:, :, None] > 0) & (
        before[:, :, None] == jnp.arange(capacity, dtype=jnp.int32)[None, None, :]
    )
    token_no = jnp.arange(rows_dev, dtype=jnp.float32)[:, None, None]
    src_of = jnp.sum(jnp.where(in_slot, token_no + 1.0, 0.0), axis=0) - 1.0
    weight_te = jnp.sum(jnp.where(chosen, combine[:, :, None], 0.0), axis=1)
    w_of = jnp.sum(jnp.where(in_slot, weight_te[:, :, None], 0.0), axis=0)
    table = jnp.stack((src_of,) + split3(w_of)).astype(jnp.bfloat16)
    extra = 16
    table = jnp.pad(table.reshape(-1), (0, extra * model_width - 4 * slots))
    packed = jnp.concatenate([tokens, table.reshape(extra, model_width)], axis=0)
    block = rows_dev + extra

    tok_g = lax.all_gather(packed, "ez", axis=0, tiled=True)
    cot_g = lax.all_gather(cotangent, "ez", axis=0, tiled=True)
    table_g = tok_g.reshape(n_z, block, model_width)[:, rows_dev:].reshape(n_z, -1)
    table_g = table_g[:, : 4 * slots].reshape(n_z, 4, expert_count, capacity)
    z_me = lax.axis_index("ez")
    mine = lax.dynamic_slice_in_dim(table_g, z_me * n_y, n_y, axis=2).astype(jnp.float32)
    mine = jnp.transpose(mine, (1, 2, 0, 3))
    src_tok = mine[0].astype(jnp.int32)
    src_w = (mine[1] + mine[2]) + mine[3]
    valid = src_tok >= 0
    z_of = jnp.arange(n_z, dtype=jnp.int32)[None, :, None]
    at_packed = jnp.where(valid, src_tok + z_of * block, -1).reshape(-1)
    at_cot = jnp.where(valid, src_tok + z_of * rows_dev, -1).reshape(-1)
    send_rows = select_rows(at_packed, tok_g).astype(jnp.bfloat16)

    rows_flat = lax.all_to_all(send_rows, "ey", split_axis=0, concat_axis=0, tiled=True)
    gate_e = w_gate[0]
    up_e = w_up[0]
    down_e = w_down[0]
    tangent_e = tangent_gate[0]
    term, factor = forward_part(rows_flat, gate_e, up_e, down_e, tangent_e)
    returned = lax.all_to_all(term, ("ey", "ez"), split_axis=0, concat_axis=0, tiled=True)
    _, cot_g = lax.optimization_barrier((term, cot_g))
    send_scaled = (src_w.reshape(-1)[:, None] * select_rows(at_cot, cot_g)).astype(jnp.bfloat16)
    scaled_flat = shift_along_y(send_scaled, n_y)
    coeff = backward_part(scaled_flat, down_e, factor)
    partial_hvp = lax.dot_general(
        rows_flat, coeff, (((0,), (0,)), ((), ())), preferred_element_type=jnp.float32
    )
    hvp_gate = lax.psum_scatter(partial_hvp, "dp", scatter_dimension=0, tiled=True)
    back_at = ((expert_ids % n_y) * n_z + expert_ids // n_y) * capacity + slot_pos
    at_slot = back_at[:, :, None] == jnp.arange(slots, dtype=jnp.int32)[None, None, :]
    output_tangent = jnp.zeros((rows_dev, model_width), jnp.float32)
    for piece in split3(combine):
        spread = jnp.sum(jnp.where(at_slot, piece[:, :, None], 0.0), axis=1).astype(jnp.bfloat16)
        output_tangent = output_tangent + jnp.dot(spread, returned, preferred_element_type=jnp.float32)
    return (hvp_gate[None], output_tangent.astype(jnp.bfloat16))


def y_size(mesh):
    column = mesh.devices[0]
    try:
        return len({int(d.coords[1]) for d in column})
    except Exception:
        return 4


def solution(mesh):
    n_dp, n_expert = mesh.devices.shape
    n_y = y_size(mesh)
    mesh3 = Mesh(mesh.devices.reshape(n_dp, n_expert // n_y, n_y), ("dp", "ez", "ey"))
    rows = P(("dp", "ez", "ey"), None)
    weights = P(("ez", "ey"), None, None)
    placed = (rows, rows, rows, rows, weights, weights, weights, weights)
    return jax.shard_map(
        per_device,
        mesh=mesh3,
        in_specs=placed,
        out_specs=(P(("ez", "ey"), "dp", None), rows),
        check_vma=False,
    )
```

```python
import jax
import jax.numpy as jnp
import numpy as np
from jax import lax
from jax.sharding import Mesh
from jax.sharding import PartitionSpec as P


def silu_derivs(gate_act):
    squash = jax.nn.sigmoid(gate_act)
    first = squash * (1.0 + gate_act * (1.0 - squash))
    second = squash * (1.0 - squash) * (2.0 + gate_act * (1.0 - 2.0 * squash))
    return (first, second)


def forward_part(rows_flat, gate_e, up_e, down_e, tangent_e, blocks):
    gate_act = jnp.dot(rows_flat, gate_e, preferred_element_type=jnp.float32)
    up_act = jnp.dot(rows_flat, up_e, preferred_element_type=jnp.float32)
    gate_dot = jnp.dot(rows_flat, tangent_e, preferred_element_type=jnp.float32)
    first, second = silu_derivs(gate_act)
    lifted = (first * gate_dot * up_act).astype(jnp.bfloat16)
    term = lax.dot_general(
        lifted.reshape(blocks + (lifted.shape[-1],)),
        down_e,
        (((2,), (0,)), ((), ())),
        preferred_element_type=jnp.float32,
    ).astype(jnp.bfloat16)
    return (term, up_act * second * gate_dot)


def backward_part(scaled_flat, down_e, factor):
    back_hidden = lax.dot_general(
        scaled_flat, down_e, (((1,), (1,)), ((), ())), preferred_element_type=jnp.float32
    )
    return (back_hidden * factor).astype(jnp.bfloat16)


def split3(value):
    hi = lax.reduce_precision(value, exponent_bits=8, mantissa_bits=7)
    rest = value - hi
    mid = lax.reduce_precision(rest, exponent_bits=8, mantissa_bits=7)
    return (hi, mid, rest - mid)


def select_rows(index, source):
    picks = (index[:, None] == jnp.arange(source.shape[0], dtype=jnp.int32)[None, :]).astype(source.dtype)
    return jnp.dot(picks, source, preferred_element_type=jnp.float32)


def shift_along_y(send, n_y):
    chunks = send.reshape(n_y, -1, send.shape[-1])
    me = lax.axis_index("ey")
    got = jnp.zeros_like(chunks)
    got = lax.dynamic_update_index_in_dim(got, lax.dynamic_index_in_dim(chunks, me, 0, False), me, 0)
    for shift in range(1, n_y):
        out = lax.dynamic_index_in_dim(chunks, (me + shift) % n_y, 0, False)
        moved = lax.ppermute(out, "ey", perm=[(i, (i + shift) % n_y) for i in range(n_y)])
        got = lax.dynamic_update_index_in_dim(got, moved, (me + n_y - shift) % n_y, 0)
    return got.reshape(send.shape)


def per_device(tokens, cotangent, expert_ids, combine, w_gate, w_up, w_down, tangent_gate):
    n_z = lax.axis_size("ez")
    n_y = lax.axis_size("ey")
    expert_count = n_z * n_y
    rows_dev, top_count = expert_ids.shape
    model_width = tokens.shape[1]
    capacity = rows_dev * top_count * 9 // (8 * expert_count)
    owners = jnp.arange(expert_count, dtype=jnp.int32)
    chosen = expert_ids[:, :, None] == owners[None, None, :]
    matches = chosen.astype(jnp.int32)
    named_count = jnp.sum(matches, axis=1)
    before = jnp.cumsum(named_count, axis=0) - named_count
    slot_pos = jnp.sum(before[:, None, :] * matches, axis=2)
    slots = expert_count * capacity
    in_slot = (named_count[:, :, None] > 0) & (
        before[:, :, None] == jnp.arange(capacity, dtype=jnp.int32)[None, None, :]
    )
    token_no = jnp.arange(rows_dev, dtype=jnp.float32)[:, None, None]
    src_of = jnp.sum(jnp.where(in_slot, token_no + 1.0, 0.0), axis=0) - 1.0
    weight_te = jnp.sum(jnp.where(chosen, combine[:, :, None], 0.0), axis=1)
    w_of = jnp.sum(jnp.where(in_slot, weight_te[:, :, None], 0.0), axis=0)
    table = jnp.stack((src_of,) + split3(w_of)).astype(jnp.bfloat16)
    extra = 16
    table = jnp.pad(table.reshape(-1), (0, extra * model_width - 4 * slots))
    packed = jnp.concatenate([tokens, table.reshape(extra, model_width)], axis=0)
    block = rows_dev + extra

    tok_g = lax.all_gather(packed, "ez", axis=0, tiled=True)
    cot_g = lax.all_gather(cotangent, "ez", axis=0, tiled=True)
    table_g = tok_g.reshape(n_z, block, model_width)[:, rows_dev:].reshape(n_z, -1)
    table_g = table_g[:, : 4 * slots].reshape(n_z, 4, expert_count, capacity)
    z_me = lax.axis_index("ez")
    mine = lax.dynamic_slice_in_dim(table_g, z_me * n_y, n_y, axis=2).astype(jnp.float32)
    mine = jnp.transpose(mine, (1, 2, 0, 3))
    src_tok = mine[0].astype(jnp.int32)
    src_w = (mine[1] + mine[2]) + mine[3]
    valid = src_tok >= 0
    z_of = jnp.arange(n_z, dtype=jnp.int32)[None, :, None]
    at_packed = jnp.where(valid, src_tok + z_of * block, -1).reshape(-1)
    at_cot = jnp.where(valid, src_tok + z_of * rows_dev, -1).reshape(-1)
    send_rows = select_rows(at_packed, tok_g).astype(jnp.bfloat16)

    rows_flat = lax.all_to_all(send_rows, "ey", split_axis=0, concat_axis=0, tiled=True)
    gate_e = w_gate[0]
    up_e = w_up[0]
    down_e = w_down[0]
    tangent_e = tangent_gate[0]
    send_scaled = (src_w.reshape(-1)[:, None] * select_rows(at_cot, cot_g)).astype(jnp.bfloat16)
    term, factor = forward_part(rows_flat, gate_e, up_e, down_e, tangent_e, (expert_count, capacity))
    returned = lax.all_to_all(term, ("ey", "ez"), split_axis=0, concat_axis=0, tiled=True)
    _, send_scaled = lax.optimization_barrier((term, send_scaled))
    scaled_flat = shift_along_y(send_scaled, n_y)
    coeff = backward_part(scaled_flat, down_e, factor)
    partial_hvp = lax.dot_general(
        rows_flat, coeff, (((0,), (0,)), ((), ())), preferred_element_type=jnp.float32
    )
    hvp_gate = lax.psum_scatter(partial_hvp, "dp", scatter_dimension=0, tiled=True)
    back_at = ((expert_ids % n_y) * n_z + expert_ids // n_y) * capacity + slot_pos
    at_slot = back_at[:, :, None] == jnp.arange(slots, dtype=jnp.int32)[None, None, :]
    output_tangent = jnp.zeros((rows_dev, model_width), jnp.float32)
    for piece in split3(combine):
        spread = jnp.sum(jnp.where(at_slot, piece[:, :, None], 0.0), axis=1).astype(jnp.bfloat16)
        output_tangent = output_tangent + lax.dot_general(
            spread.reshape(rows_dev, expert_count, capacity),
            returned,
            (((1, 2), (0, 1)), ((), ())),
            preferred_element_type=jnp.float32,
        )
    return (hvp_gate[None], output_tangent.astype(jnp.bfloat16))


def y_size(mesh):
    column = mesh.devices[0]
    try:
        return len({int(d.coords[1]) for d in column})
    except Exception:
        return 4


def solution(mesh):
    n_dp, n_expert = mesh.devices.shape
    n_y = y_size(mesh)
    mesh3 = Mesh(mesh.devices.reshape(n_dp, n_expert // n_y, n_y), ("dp", "ez", "ey"))
    rows = P(("dp", "ez", "ey"), None)
    weights = P(("ez", "ey"), None, None)
    placed = (rows, rows, rows, rows, weights, weights, weights, weights)
    return jax.shard_map(
        per_device,
        mesh=mesh3,
        in_specs=placed,
        out_specs=(P(("ez", "ey"), "dp", None), rows),
        check_vma=False,
    )
```

```python
import jax
import jax.numpy as jnp
import numpy as np
from jax import lax
from jax.sharding import Mesh
from jax.sharding import PartitionSpec as P


def silu_derivs(gate_act):
    squash = jax.nn.sigmoid(gate_act)
    first = squash * (1.0 + gate_act * (1.0 - squash))
    second = squash * (1.0 - squash) * (2.0 + gate_act * (1.0 - 2.0 * squash))
    return (first, second)


def forward_part(rows_flat, gate_e, up_e, down_e, tangent_e, blocks):
    gate_act = jnp.dot(rows_flat, gate_e, preferred_element_type=jnp.float32)
    up_act = jnp.dot(rows_flat, up_e, preferred_element_type=jnp.float32)
    gate_dot = jnp.dot(rows_flat, tangent_e, preferred_element_type=jnp.float32)
    first, second = silu_derivs(gate_act)
    lifted = (first * gate_dot * up_act).astype(jnp.bfloat16)
    term = lax.dot_general(
        lifted.reshape(blocks + (lifted.shape[-1],)),
        down_e,
        (((2,), (0,)), ((), ())),
        preferred_element_type=jnp.float32,
    ).astype(jnp.bfloat16)
    return (term, up_act * second * gate_dot)


def backward_part(scaled_flat, down_e, factor):
    back_hidden = lax.dot_general(
        scaled_flat, down_e, (((1,), (1,)), ((), ())), preferred_element_type=jnp.float32
    )
    return (back_hidden * factor).astype(jnp.bfloat16)


def split3(value):
    hi = lax.reduce_precision(value, exponent_bits=8, mantissa_bits=7)
    rest = value - hi
    mid = lax.reduce_precision(rest, exponent_bits=8, mantissa_bits=7)
    return (hi, mid, rest - mid)


def select_rows(index, source):
    picks = (index[:, None] == jnp.arange(source.shape[0], dtype=jnp.int32)[None, :]).astype(source.dtype)
    return jnp.dot(picks, source, preferred_element_type=jnp.float32)


def shift_along_y(send, n_y):
    chunks = send.reshape(n_y, -1, send.shape[-1])
    me = lax.axis_index("ey")
    got = jnp.zeros_like(chunks)
    got = lax.dynamic_update_index_in_dim(got, lax.dynamic_index_in_dim(chunks, me, 0, False), me, 0)
    for shift in range(1, n_y):
        out = lax.dynamic_index_in_dim(chunks, (me + shift) % n_y, 0, False)
        moved = lax.ppermute(out, "ey", perm=[(i, (i + shift) % n_y) for i in range(n_y)])
        got = lax.dynamic_update_index_in_dim(got, moved, (me + n_y - shift) % n_y, 0)
    return got.reshape(send.shape)


def per_device(tokens, cotangent, expert_ids, combine, w_gate, w_up, w_down, tangent_gate):
    n_z = lax.axis_size("ez")
    n_y = lax.axis_size("ey")
    expert_count = n_z * n_y
    rows_dev, top_count = expert_ids.shape
    model_width = tokens.shape[1]
    capacity = rows_dev * top_count * 9 // (8 * expert_count)
    owners = jnp.arange(expert_count, dtype=jnp.int32)
    chosen = expert_ids[:, :, None] == owners[None, None, :]
    matches = chosen.astype(jnp.int32)
    named_count = jnp.sum(matches, axis=1)
    before = jnp.cumsum(named_count, axis=0) - named_count
    slot_pos = jnp.sum(before[:, None, :] * matches, axis=2)
    slots = expert_count * capacity
    in_slot = (named_count[:, :, None] > 0) & (
        before[:, :, None] == jnp.arange(capacity, dtype=jnp.int32)[None, None, :]
    )
    token_no = jnp.arange(rows_dev, dtype=jnp.float32)[:, None, None]
    src_of = jnp.sum(jnp.where(in_slot, token_no + 1.0, 0.0), axis=0) - 1.0
    weight_te = jnp.sum(jnp.where(chosen, combine[:, :, None], 0.0), axis=1)
    w_of = jnp.sum(jnp.where(in_slot, weight_te[:, :, None], 0.0), axis=0)
    table = jnp.stack((src_of,) + split3(w_of)).astype(jnp.bfloat16)
    extra = 16
    table = jnp.pad(table.reshape(-1), (0, extra * model_width - 4 * slots))
    packed = jnp.concatenate([tokens, table.reshape(extra, model_width)], axis=0)
    block = rows_dev + extra

    tok_g = lax.all_gather(packed, "ez", axis=0, tiled=True)
    cot_g = lax.all_gather(cotangent, "ez", axis=0, tiled=True)
    table_g = tok_g.reshape(n_z, block, model_width)[:, rows_dev:].reshape(n_z, -1)
    table_g = table_g[:, : 4 * slots].reshape(n_z, 4, expert_count, capacity)
    z_me = lax.axis_index("ez")
    mine = lax.dynamic_slice_in_dim(table_g, z_me * n_y, n_y, axis=2).astype(jnp.float32)
    mine = jnp.transpose(mine, (1, 2, 0, 3))
    src_tok = mine[0].astype(jnp.int32)
    src_w = (mine[1] + mine[2]) + mine[3]
    valid = src_tok >= 0
    z_of = jnp.arange(n_z, dtype=jnp.int32)[None, :, None]
    at_packed = jnp.where(valid, src_tok + z_of * block, -1).reshape(-1)
    at_cot = jnp.where(valid, src_tok + z_of * rows_dev, -1).reshape(-1)
    send_rows = select_rows(at_packed, tok_g).astype(jnp.bfloat16)

    rows_flat = lax.all_to_all(send_rows, "ey", split_axis=0, concat_axis=0, tiled=True)
    gate_e = w_gate[0]
    up_e = w_up[0]
    down_e = w_down[0]
    tangent_e = tangent_gate[0]
    send_scaled = (src_w.reshape(-1)[:, None] * select_rows(at_cot, cot_g)).astype(jnp.bfloat16)
    term, factor = forward_part(rows_flat, gate_e, up_e, down_e, tangent_e, (expert_count, capacity))
    returned = lax.all_to_all(term, ("ey", "ez"), split_axis=0, concat_axis=0, tiled=True)
    _, send_scaled = lax.optimization_barrier((rows_flat, send_scaled))
    scaled_flat = shift_along_y(send_scaled, n_y)
    coeff = backward_part(scaled_flat, down_e, factor)
    partial_hvp = lax.dot_general(
        rows_flat, coeff, (((0,), (0,)), ((), ())), preferred_element_type=jnp.float32
    )
    hvp_gate = lax.psum_scatter(partial_hvp, "dp", scatter_dimension=0, tiled=True)
    back_at = ((expert_ids % n_y) * n_z + expert_ids // n_y) * capacity + slot_pos
    at_slot = back_at[:, :, None] == jnp.arange(slots, dtype=jnp.int32)[None, None, :]
    output_tangent = jnp.zeros((rows_dev, model_width), jnp.float32)
    for piece in split3(combine):
        spread = jnp.sum(jnp.where(at_slot, piece[:, :, None], 0.0), axis=1).astype(jnp.bfloat16)
        output_tangent = output_tangent + lax.dot_general(
            spread.reshape(rows_dev, expert_count, capacity),
            returned,
            (((1, 2), (0, 1)), ((), ())),
            preferred_element_type=jnp.float32,
        )
    return (hvp_gate[None], output_tangent.astype(jnp.bfloat16))


def y_size(mesh):
    column = mesh.devices[0]
    try:
        return len({int(d.coords[1]) for d in column})
    except Exception:
        return 4


def solution(mesh):
    n_dp, n_expert = mesh.devices.shape
    n_y = y_size(mesh)
    mesh3 = Mesh(mesh.devices.reshape(n_dp, n_expert // n_y, n_y), ("dp", "ez", "ey"))
    rows = P(("dp", "ez", "ey"), None)
    weights = P(("ez", "ey"), None, None)
    placed = (rows, rows, rows, rows, weights, weights, weights, weights)
    return jax.shard_map(
        per_device,
        mesh=mesh3,
        in_specs=placed,
        out_specs=(P(("ez", "ey"), "dp", None), rows),
        check_vma=False,
    )
```

```python
import jax
import jax.numpy as jnp
import numpy as np
from jax import lax
from jax.sharding import Mesh
from jax.sharding import PartitionSpec as P


def silu_derivs(gate_act):
    squash = jax.nn.sigmoid(gate_act)
    first = squash * (1.0 + gate_act * (1.0 - squash))
    second = squash * (1.0 - squash) * (2.0 + gate_act * (1.0 - 2.0 * squash))
    return (first, second)


def forward_part(halves, gate_e, up_e, down_e, tangent_e, blocks):
    cut = halves[0].shape[1]

    def project(weight):
        parts = [
            jnp.dot(h, weight[i * cut : (i + 1) * cut], preferred_element_type=jnp.float32)
            for i, h in enumerate(halves)
        ]
        return parts[0] + parts[1]

    gate_act = project(gate_e)
    up_act = project(up_e)
    gate_dot = project(tangent_e)
    first, second = silu_derivs(gate_act)
    lifted = (first * gate_dot * up_act).astype(jnp.bfloat16)
    term = lax.dot_general(
        lifted.reshape(blocks + (lifted.shape[-1],)),
        down_e,
        (((2,), (0,)), ((), ())),
        preferred_element_type=jnp.float32,
    ).astype(jnp.bfloat16)
    return (term, up_act * second * gate_dot)


def backward_part(scaled_flat, down_e, factor):
    back_hidden = lax.dot_general(
        scaled_flat, down_e, (((1,), (1,)), ((), ())), preferred_element_type=jnp.float32
    )
    return (back_hidden * factor).astype(jnp.bfloat16)


def split3(value):
    hi = lax.reduce_precision(value, exponent_bits=8, mantissa_bits=7)
    rest = value - hi
    mid = lax.reduce_precision(rest, exponent_bits=8, mantissa_bits=7)
    return (hi, mid, rest - mid)


def select_rows(index, source):
    picks = (index[:, None] == jnp.arange(source.shape[0], dtype=jnp.int32)[None, :]).astype(source.dtype)
    return jnp.dot(picks, source, preferred_element_type=jnp.float32)


def shift_along_y(send, n_y):
    chunks = send.reshape(n_y, -1, send.shape[-1])
    me = lax.axis_index("ey")
    got = jnp.zeros_like(chunks)
    got = lax.dynamic_update_index_in_dim(got, lax.dynamic_index_in_dim(chunks, me, 0, False), me, 0)
    for shift in range(1, n_y):
        out = lax.dynamic_index_in_dim(chunks, (me + shift) % n_y, 0, False)
        moved = lax.ppermute(out, "ey", perm=[(i, (i + shift) % n_y) for i in range(n_y)])
        got = lax.dynamic_update_index_in_dim(got, moved, (me + n_y - shift) % n_y, 0)
    return got.reshape(send.shape)


def per_device(tokens, cotangent, expert_ids, combine, w_gate, w_up, w_down, tangent_gate):
    n_z = lax.axis_size("ez")
    n_y = lax.axis_size("ey")
    expert_count = n_z * n_y
    rows_dev, top_count = expert_ids.shape
    model_width = tokens.shape[1]
    capacity = rows_dev * top_count * 9 // (8 * expert_count)
    owners = jnp.arange(expert_count, dtype=jnp.int32)
    chosen = expert_ids[:, :, None] == owners[None, None, :]
    matches = chosen.astype(jnp.int32)
    named_count = jnp.sum(matches, axis=1)
    before = jnp.cumsum(named_count, axis=0) - named_count
    slot_pos = jnp.sum(before[:, None, :] * matches, axis=2)
    slots = expert_count * capacity
    in_slot = (named_count[:, :, None] > 0) & (
        before[:, :, None] == jnp.arange(capacity, dtype=jnp.int32)[None, None, :]
    )
    token_no = jnp.arange(rows_dev, dtype=jnp.float32)[:, None, None]
    src_of = jnp.sum(jnp.where(in_slot, token_no + 1.0, 0.0), axis=0) - 1.0
    weight_te = jnp.sum(jnp.where(chosen, combine[:, :, None], 0.0), axis=1)
    w_of = jnp.sum(jnp.where(in_slot, weight_te[:, :, None], 0.0), axis=0)
    table = jnp.stack((src_of,) + split3(w_of)).astype(jnp.bfloat16)
    extra = 16
    cut = model_width // 2
    table = jnp.pad(table.reshape(-1), (0, extra * cut - 4 * slots))
    packed = jnp.concatenate([tokens[:, :cut], table.reshape(extra, cut)], axis=0)
    block = rows_dev + extra

    tok_a = lax.all_gather(packed, "ez", axis=0, tiled=True)
    tok_b = lax.all_gather(tokens[:, cut:], "ez", axis=0, tiled=True)
    cot_g = lax.all_gather(cotangent, "ez", axis=0, tiled=True)
    table_g = tok_a.reshape(n_z, block, cut)[:, rows_dev:].reshape(n_z, -1)
    table_g = table_g[:, : 4 * slots].reshape(n_z, 4, expert_count, capacity)
    z_me = lax.axis_index("ez")
    mine = lax.dynamic_slice_in_dim(table_g, z_me * n_y, n_y, axis=2).astype(jnp.float32)
    mine = jnp.transpose(mine, (1, 2, 0, 3))
    src_tok = mine[0].astype(jnp.int32)
    src_w = (mine[1] + mine[2]) + mine[3]
    valid = src_tok >= 0
    z_of = jnp.arange(n_z, dtype=jnp.int32)[None, :, None]
    at_packed = jnp.where(valid, src_tok + z_of * block, -1).reshape(-1)
    at_cot = jnp.where(valid, src_tok + z_of * rows_dev, -1).reshape(-1)
    send_a = select_rows(at_packed, tok_a).astype(jnp.bfloat16)
    send_b = select_rows(at_cot, tok_b).astype(jnp.bfloat16)

    rows_a = lax.all_to_all(send_a, "ey", split_axis=0, concat_axis=0, tiled=True)
    rows_b = lax.all_to_all(send_b, "ey", split_axis=0, concat_axis=0, tiled=True)
    gate_e = w_gate[0]
    up_e = w_up[0]
    down_e = w_down[0]
    tangent_e = tangent_gate[0]
    send_scaled = (src_w.reshape(-1)[:, None] * select_rows(at_cot, cot_g)).astype(jnp.bfloat16)
    term, factor = forward_part((rows_a, rows_b), gate_e, up_e, down_e, tangent_e, (expert_count, capacity))
    returned = lax.all_to_all(term, ("ey", "ez"), split_axis=0, concat_axis=0, tiled=True)
    _, send_scaled = lax.optimization_barrier((rows_b, send_scaled))
    scaled_flat = shift_along_y(send_scaled, n_y)
    coeff = backward_part(scaled_flat, down_e, factor)
    partial_hvp = jnp.concatenate(
        [
            lax.dot_general(h, coeff, (((0,), (0,)), ((), ())), preferred_element_type=jnp.float32)
            for h in (rows_a, rows_b)
        ],
        axis=0,
    )
    hvp_gate = lax.psum_scatter(partial_hvp, "dp", scatter_dimension=0, tiled=True)
    back_at = ((expert_ids % n_y) * n_z + expert_ids // n_y) * capacity + slot_pos
    at_slot = back_at[:, :, None] == jnp.arange(slots, dtype=jnp.int32)[None, None, :]
    output_tangent = jnp.zeros((rows_dev, model_width), jnp.float32)
    for piece in split3(combine):
        spread = jnp.sum(jnp.where(at_slot, piece[:, :, None], 0.0), axis=1).astype(jnp.bfloat16)
        output_tangent = output_tangent + lax.dot_general(
            spread.reshape(rows_dev, expert_count, capacity),
            returned,
            (((1, 2), (0, 1)), ((), ())),
            preferred_element_type=jnp.float32,
        )
    return (hvp_gate[None], output_tangent.astype(jnp.bfloat16))


def y_size(mesh):
    column = mesh.devices[0]
    try:
        return len({int(d.coords[1]) for d in column})
    except Exception:
        return 4


def solution(mesh):
    n_dp, n_expert = mesh.devices.shape
    n_y = y_size(mesh)
    mesh3 = Mesh(mesh.devices.reshape(n_dp, n_expert // n_y, n_y), ("dp", "ez", "ey"))
    rows = P(("dp", "ez", "ey"), None)
    weights = P(("ez", "ey"), None, None)
    placed = (rows, rows, rows, rows, weights, weights, weights, weights)
    return jax.shard_map(
        per_device,
        mesh=mesh3,
        in_specs=placed,
        out_specs=(P(("ez", "ey"), "dp", None), rows),
        check_vma=False,
    )
```

```python
import jax
import jax.numpy as jnp
import numpy as np
from jax import lax
from jax.sharding import Mesh
from jax.sharding import PartitionSpec as P


def silu_derivs(gate_act):
    squash = jax.nn.sigmoid(gate_act)
    first = squash * (1.0 + gate_act * (1.0 - squash))
    second = squash * (1.0 - squash) * (2.0 + gate_act * (1.0 - 2.0 * squash))
    return (first, second)


def forward_part(rows_flat, gate_e, up_e, down_e, tangent_e, blocks):
    gate_act = jnp.dot(rows_flat, gate_e, preferred_element_type=jnp.float32)
    up_act = jnp.dot(rows_flat, up_e, preferred_element_type=jnp.float32)
    gate_dot = jnp.dot(rows_flat, tangent_e, preferred_element_type=jnp.float32)
    first, second = silu_derivs(gate_act)
    lifted = (first * gate_dot * up_act).astype(jnp.bfloat16)
    term = lax.dot_general(
        lifted.reshape(blocks + (lifted.shape[-1],)),
        down_e,
        (((2,), (0,)), ((), ())),
        preferred_element_type=jnp.float32,
    ).astype(jnp.bfloat16)
    return (term, up_act * second * gate_dot)


def backward_part(scaled_flat, down_e, factor):
    back_hidden = lax.dot_general(
        scaled_flat, down_e, (((1,), (1,)), ((), ())), preferred_element_type=jnp.float32
    )
    return (back_hidden * factor).astype(jnp.bfloat16)


def split3(value):
    hi = lax.reduce_precision(value, exponent_bits=8, mantissa_bits=7)
    rest = value - hi
    mid = lax.reduce_precision(rest, exponent_bits=8, mantissa_bits=7)
    return (hi, mid, rest - mid)


def select_rows(index, source):
    picks = (index[:, None] == jnp.arange(source.shape[0], dtype=jnp.int32)[None, :]).astype(source.dtype)
    return jnp.dot(picks, source, preferred_element_type=jnp.float32)


def shift_along_y(send, n_y):
    chunks = send.reshape(n_y, -1, send.shape[-1])
    me = lax.axis_index("ey")
    got = jnp.zeros_like(chunks)
    got = lax.dynamic_update_index_in_dim(got, lax.dynamic_index_in_dim(chunks, me, 0, False), me, 0)
    for shift in range(1, n_y):
        out = lax.dynamic_index_in_dim(chunks, (me + shift) % n_y, 0, False)
        moved = lax.ppermute(out, "ey", perm=[(i, (i + shift) % n_y) for i in range(n_y)])
        got = lax.dynamic_update_index_in_dim(got, moved, (me + n_y - shift) % n_y, 0)
    return got.reshape(send.shape)


def per_device(tokens, cotangent, expert_ids, combine, w_gate, w_up, w_down, tangent_gate):
    n_z = lax.axis_size("ez")
    n_y = lax.axis_size("ey")
    expert_count = n_z * n_y
    rows_dev, top_count = expert_ids.shape
    model_width = tokens.shape[1]
    capacity = rows_dev * top_count * 9 // (8 * expert_count)
    owners = jnp.arange(expert_count, dtype=jnp.int32)
    chosen = expert_ids[:, :, None] == owners[None, None, :]
    matches = chosen.astype(jnp.int32)
    named_count = jnp.sum(matches, axis=1)
    before = jnp.cumsum(named_count, axis=0) - named_count
    slot_pos = jnp.sum(before[:, None, :] * matches, axis=2)
    slots = expert_count * capacity
    in_slot = (named_count[:, :, None] > 0) & (
        before[:, :, None] == jnp.arange(capacity, dtype=jnp.int32)[None, None, :]
    )
    token_no = jnp.arange(rows_dev, dtype=jnp.float32)[:, None, None]
    src_of = jnp.sum(jnp.where(in_slot, token_no + 1.0, 0.0), axis=0) - 1.0
    weight_te = jnp.sum(jnp.where(chosen, combine[:, :, None], 0.0), axis=1)
    w_of = jnp.sum(jnp.where(in_slot, weight_te[:, :, None], 0.0), axis=0)
    table = jnp.stack((src_of,) + split3(w_of)).astype(jnp.bfloat16)
    extra = 16
    table = jnp.pad(table.reshape(-1), (0, extra * model_width - 4 * slots))
    packed = jnp.concatenate([tokens, table.reshape(extra, model_width)], axis=0)
    block = rows_dev + extra

    tok_g = lax.all_gather(packed, "ez", axis=0, tiled=True)
    cot_g = lax.all_gather(cotangent, "ez", axis=0, tiled=True)
    table_g = tok_g.reshape(n_z, block, model_width)[:, rows_dev:].reshape(n_z, -1)
    table_g = table_g[:, : 4 * slots].reshape(n_z, 4, expert_count, capacity)
    z_me = lax.axis_index("ez")
    mine = lax.dynamic_slice_in_dim(table_g, z_me * n_y, n_y, axis=2).astype(jnp.float32)
    mine = jnp.transpose(mine, (1, 2, 0, 3))
    src_tok = mine[0].astype(jnp.int32)
    src_w = (mine[1] + mine[2]) + mine[3]
    valid = src_tok >= 0
    z_of = jnp.arange(n_z, dtype=jnp.int32)[None, :, None]
    at_packed = jnp.where(valid, src_tok + z_of * block, -1)
    at_cot = jnp.where(valid, src_tok + z_of * rows_dev, -1)
    half = capacity // 2
    parts = ((0, half), (half, capacity))
    gate_e = w_gate[0]
    up_e = w_up[0]
    down_e = w_down[0]
    tangent_e = tangent_gate[0]

    send_rows = [select_rows(at_packed[:, :, a:b].reshape(-1), tok_g).astype(jnp.bfloat16) for a, b in parts]
    by_chunk = lambda table: table.reshape(n_y, n_z, 2, half).transpose(0, 2, 1, 3).reshape(-1)
    send_scaled = (
        by_chunk(src_w)[:, None] * select_rows(by_chunk(at_cot), cot_g)
    ).astype(jnp.bfloat16)
    rows_0 = lax.all_to_all(send_rows[0], "ey", split_axis=0, concat_axis=0, tiled=True)
    _, send_1 = lax.optimization_barrier((rows_0, send_rows[1]))
    rows_1 = shift_along_y(send_1, n_y)
    rows = (rows_0, rows_1)
    terms, factors = [], []
    for c, (a, b) in enumerate(parts):
        term, factor = forward_part(rows[c], gate_e, up_e, down_e, tangent_e, (expert_count, b - a))
        terms.append(term)
        factors.append(factor)
    returned = [
        lax.all_to_all(t, ("ey", "ez"), split_axis=0, concat_axis=0, tiled=True) for t in terms
    ]
    _, scaled_send = lax.optimization_barrier((rows_1, send_scaled))
    scaled_all = shift_along_y(scaled_send, n_y)
    partial_hvp = jnp.zeros((model_width, factors[0].shape[1]), jnp.float32)
    for c in range(2):
        count = rows[c].shape[0]
        coeff = backward_part(scaled_all_chunk(scaled_all, n_y, c, count), down_e, factors[c])
        partial_hvp = partial_hvp + lax.dot_general(
            rows[c], coeff, (((0,), (0,)), ((), ())), preferred_element_type=jnp.float32
        )
    hvp_gate = lax.psum_scatter(partial_hvp, "dp", scatter_dimension=0, tiled=True)
    output_tangent = jnp.zeros((rows_dev, model_width), jnp.float32)
    source_at = (expert_ids % n_y) * n_z + expert_ids // n_y
    for c, (a, b) in enumerate(parts):
        width = b - a
        inside = (slot_pos >= a) & (slot_pos < b)
        back_at = jnp.where(inside, source_at * width + slot_pos - a, -1)
        at_slot = back_at[:, :, None] == jnp.arange(expert_count * width, dtype=jnp.int32)[None, None, :]
        for piece in split3(combine):
            spread = jnp.sum(jnp.where(at_slot, piece[:, :, None], 0.0), axis=1).astype(jnp.bfloat16)
            output_tangent = output_tangent + lax.dot_general(
                spread.reshape(rows_dev, expert_count, width),
                returned[c],
                (((1, 2), (0, 1)), ((), ())),
                preferred_element_type=jnp.float32,
            )
    return (hvp_gate[None], output_tangent.astype(jnp.bfloat16))


def scaled_all_chunk(scaled_all, n_y, c, count):
    per_y = scaled_all.reshape(n_y, 2, count // n_y, scaled_all.shape[-1])
    return per_y[:, c].reshape(count, scaled_all.shape[-1])


def y_size(mesh):
    column = mesh.devices[0]
    try:
        return len({int(d.coords[1]) for d in column})
    except Exception:
        return 4


def solution(mesh):
    n_dp, n_expert = mesh.devices.shape
    n_y = y_size(mesh)
    mesh3 = Mesh(mesh.devices.reshape(n_dp, n_expert // n_y, n_y), ("dp", "ez", "ey"))
    rows = P(("dp", "ez", "ey"), None)
    weights = P(("ez", "ey"), None, None)
    placed = (rows, rows, rows, rows, weights, weights, weights, weights)
    return jax.shard_map(
        per_device,
        mesh=mesh3,
        in_specs=placed,
        out_specs=(P(("ez", "ey"), "dp", None), rows),
        check_vma=False,
    )
```

```python
import jax
import jax.numpy as jnp
import numpy as np
from jax import lax
from jax.sharding import Mesh
from jax.sharding import PartitionSpec as P


def silu_derivs(gate_act):
    squash = jax.nn.sigmoid(gate_act)
    first = squash * (1.0 + gate_act * (1.0 - squash))
    second = squash * (1.0 - squash) * (2.0 + gate_act * (1.0 - 2.0 * squash))
    return (first, second)


def forward_part(rows_flat, gate_e, up_e, down_e, tangent_e, blocks):
    gate_act = jnp.dot(rows_flat, gate_e, preferred_element_type=jnp.float32)
    up_act = jnp.dot(rows_flat, up_e, preferred_element_type=jnp.float32)
    gate_dot = jnp.dot(rows_flat, tangent_e, preferred_element_type=jnp.float32)
    first, second = silu_derivs(gate_act)
    lifted = (first * gate_dot * up_act).astype(jnp.bfloat16)
    term = lax.dot_general(
        lifted.reshape(blocks + (lifted.shape[-1],)),
        down_e,
        (((2,), (0,)), ((), ())),
        preferred_element_type=jnp.float32,
    ).astype(jnp.bfloat16)
    return (term, up_act * second * gate_dot)


def backward_part(scaled_flat, down_e, factor):
    back_hidden = lax.dot_general(
        scaled_flat, down_e, (((1,), (1,)), ((), ())), preferred_element_type=jnp.float32
    )
    return (back_hidden * factor).astype(jnp.bfloat16)


def split3(value):
    hi = lax.reduce_precision(value, exponent_bits=8, mantissa_bits=7)
    rest = value - hi
    mid = lax.reduce_precision(rest, exponent_bits=8, mantissa_bits=7)
    return (hi, mid, rest - mid)


def select_rows(index, source):
    picks = (index[:, None] == jnp.arange(source.shape[0], dtype=jnp.int32)[None, :]).astype(source.dtype)
    return jnp.dot(picks, source, preferred_element_type=jnp.float32)


def shift_along_y(send, n_y):
    chunks = send.reshape(n_y, -1, send.shape[-1])
    me = lax.axis_index("ey")
    got = jnp.zeros_like(chunks)
    got = lax.dynamic_update_index_in_dim(got, lax.dynamic_index_in_dim(chunks, me, 0, False), me, 0)
    for shift in range(1, n_y):
        out = lax.dynamic_index_in_dim(chunks, (me + shift) % n_y, 0, False)
        moved = lax.ppermute(out, "ey", perm=[(i, (i + shift) % n_y) for i in range(n_y)])
        got = lax.dynamic_update_index_in_dim(got, moved, (me + n_y - shift) % n_y, 0)
    return got.reshape(send.shape)


def per_device(tokens, cotangent, expert_ids, combine, w_gate, w_up, w_down, tangent_gate):
    n_z = lax.axis_size("ez")
    n_y = lax.axis_size("ey")
    expert_count = n_z * n_y
    rows_dev, top_count = expert_ids.shape
    model_width = tokens.shape[1]
    capacity = rows_dev * top_count * 9 // (8 * expert_count)
    owners = jnp.arange(expert_count, dtype=jnp.int32)
    chosen = expert_ids[:, :, None] == owners[None, None, :]
    matches = chosen.astype(jnp.int32)
    named_count = jnp.sum(matches, axis=1)
    before = jnp.cumsum(named_count, axis=0) - named_count
    slot_pos = jnp.sum(before[:, None, :] * matches, axis=2)
    slots = expert_count * capacity
    in_slot = (named_count[:, :, None] > 0) & (
        before[:, :, None] == jnp.arange(capacity, dtype=jnp.int32)[None, None, :]
    )
    token_no = jnp.arange(rows_dev, dtype=jnp.float32)[:, None, None]
    src_of = jnp.sum(jnp.where(in_slot, token_no + 1.0, 0.0), axis=0) - 1.0
    weight_te = jnp.sum(jnp.where(chosen, combine[:, :, None], 0.0), axis=1)
    w_of = jnp.sum(jnp.where(in_slot, weight_te[:, :, None], 0.0), axis=0)
    table = jnp.stack((src_of,) + split3(w_of)).astype(jnp.bfloat16)
    extra = 16
    table = jnp.pad(table.reshape(-1), (0, extra * model_width - 4 * slots))
    packed = jnp.concatenate([tokens, table.reshape(extra, model_width)], axis=0)
    block = rows_dev + extra

    tok_g = lax.all_gather(packed, "ez", axis=0, tiled=True)
    cot_g = lax.all_gather(cotangent, "ez", axis=0, tiled=True)
    table_g = tok_g.reshape(n_z, block, model_width)[:, rows_dev:].reshape(n_z, -1)
    table_g = table_g[:, : 4 * slots].reshape(n_z, 4, expert_count, capacity)
    z_me = lax.axis_index("ez")
    mine = lax.dynamic_slice_in_dim(table_g, z_me * n_y, n_y, axis=2).astype(jnp.float32)
    mine = jnp.transpose(mine, (1, 2, 0, 3))
    src_tok = mine[0].astype(jnp.int32)
    src_w = (mine[1] + mine[2]) + mine[3]
    valid = src_tok >= 0
    z_of = jnp.arange(n_z, dtype=jnp.int32)[None, :, None]
    at_packed = jnp.where(valid, src_tok + z_of * block, -1)
    at_cot = jnp.where(valid, src_tok + z_of * rows_dev, -1)
    half = capacity // 2
    parts = ((0, half), (half, capacity))
    gate_e = w_gate[0]
    up_e = w_up[0]
    down_e = w_down[0]
    tangent_e = tangent_gate[0]

    send_rows = [select_rows(at_packed[:, :, a:b].reshape(-1), tok_g).astype(jnp.bfloat16) for a, b in parts]
    by_chunk = lambda table: table.reshape(n_y, n_z, 2, half).transpose(0, 2, 1, 3).reshape(-1)
    send_scaled = (
        by_chunk(src_w)[:, None] * select_rows(by_chunk(at_cot), cot_g)
    ).astype(jnp.bfloat16)
    rows_0 = lax.all_to_all(send_rows[0], "ey", split_axis=0, concat_axis=0, tiled=True)
    _, send_1 = lax.optimization_barrier((rows_0, send_rows[1]))
    rows_1 = shift_along_y(send_1, n_y)
    rows = (rows_0, rows_1)
    terms, factors = [], []
    for c, (a, b) in enumerate(parts):
        term, factor = forward_part(rows[c], gate_e, up_e, down_e, tangent_e, (expert_count, b - a))
        terms.append(term)
        factors.append(factor)
    returned = [
        lax.all_to_all(t, ("ey", "ez"), split_axis=0, concat_axis=0, tiled=True) for t in terms
    ]
    _, scaled_send = lax.optimization_barrier((rows_1, send_scaled))
    scaled_all = shift_along_y(scaled_send, n_y)
    _, scaled_all = lax.optimization_barrier((terms[1], scaled_all))
    partial_hvp = jnp.zeros((model_width, factors[0].shape[1]), jnp.float32)
    for c in range(2):
        count = rows[c].shape[0]
        coeff = backward_part(scaled_all_chunk(scaled_all, n_y, c, count), down_e, factors[c])
        partial_hvp = partial_hvp + lax.dot_general(
            rows[c], coeff, (((0,), (0,)), ((), ())), preferred_element_type=jnp.float32
        )
    hvp_gate = lax.psum_scatter(partial_hvp, "dp", scatter_dimension=0, tiled=True)
    output_tangent = jnp.zeros((rows_dev, model_width), jnp.float32)
    source_at = (expert_ids % n_y) * n_z + expert_ids // n_y
    for c, (a, b) in enumerate(parts):
        width = b - a
        inside = (slot_pos >= a) & (slot_pos < b)
        back_at = jnp.where(inside, source_at * width + slot_pos - a, -1)
        at_slot = back_at[:, :, None] == jnp.arange(expert_count * width, dtype=jnp.int32)[None, None, :]
        for piece in split3(combine):
            spread = jnp.sum(jnp.where(at_slot, piece[:, :, None], 0.0), axis=1).astype(jnp.bfloat16)
            output_tangent = output_tangent + lax.dot_general(
                spread.reshape(rows_dev, expert_count, width),
                returned[c],
                (((1, 2), (0, 1)), ((), ())),
                preferred_element_type=jnp.float32,
            )
    return (hvp_gate[None], output_tangent.astype(jnp.bfloat16))


def scaled_all_chunk(scaled_all, n_y, c, count):
    per_y = scaled_all.reshape(n_y, 2, count // n_y, scaled_all.shape[-1])
    return per_y[:, c].reshape(count, scaled_all.shape[-1])


def y_size(mesh):
    column = mesh.devices[0]
    try:
        return len({int(d.coords[1]) for d in column})
    except Exception:
        return 4


def solution(mesh):
    n_dp, n_expert = mesh.devices.shape
    n_y = y_size(mesh)
    mesh3 = Mesh(mesh.devices.reshape(n_dp, n_expert // n_y, n_y), ("dp", "ez", "ey"))
    rows = P(("dp", "ez", "ey"), None)
    weights = P(("ez", "ey"), None, None)
    placed = (rows, rows, rows, rows, weights, weights, weights, weights)
    return jax.shard_map(
        per_device,
        mesh=mesh3,
        in_specs=placed,
        out_specs=(P(("ez", "ey"), "dp", None), rows),
        check_vma=False,
    )
```

```python
import jax
import jax.numpy as jnp
import numpy as np
from jax import lax
from jax.sharding import Mesh
from jax.sharding import PartitionSpec as P


def silu_derivs(gate_act):
    squash = jax.nn.sigmoid(gate_act)
    first = squash * (1.0 + gate_act * (1.0 - squash))
    second = squash * (1.0 - squash) * (2.0 + gate_act * (1.0 - 2.0 * squash))
    return (first, second)


def forward_part(rows_flat, joined_e, down_e, blocks):
    hidden = down_e.shape[0]
    acts = jnp.dot(rows_flat, joined_e, preferred_element_type=jnp.float32)
    gate_act = acts[:, :hidden]
    up_act = acts[:, hidden : 2 * hidden]
    gate_dot = acts[:, 2 * hidden :]
    first, second = silu_derivs(gate_act)
    lifted = (first * gate_dot * up_act).astype(jnp.bfloat16)
    term = lax.dot_general(
        lifted.reshape(blocks + (lifted.shape[-1],)),
        down_e,
        (((2,), (0,)), ((), ())),
        preferred_element_type=jnp.float32,
    ).astype(jnp.bfloat16)
    return (term, up_act * second * gate_dot)


def backward_part(scaled_flat, down_e, factor):
    back_hidden = lax.dot_general(
        scaled_flat, down_e, (((1,), (1,)), ((), ())), preferred_element_type=jnp.float32
    )
    return (back_hidden * factor).astype(jnp.bfloat16)


def split3(value):
    hi = lax.reduce_precision(value, exponent_bits=8, mantissa_bits=7)
    rest = value - hi
    mid = lax.reduce_precision(rest, exponent_bits=8, mantissa_bits=7)
    return (hi, mid, rest - mid)


def select_rows(index, source):
    picks = (index[:, None] == jnp.arange(source.shape[0], dtype=jnp.int32)[None, :]).astype(source.dtype)
    return jnp.dot(picks, source, preferred_element_type=jnp.float32)


def shift_along_y(send, n_y):
    chunks = send.reshape(n_y, -1, send.shape[-1])
    me = lax.axis_index("ey")
    got = jnp.zeros_like(chunks)
    got = lax.dynamic_update_index_in_dim(got, lax.dynamic_index_in_dim(chunks, me, 0, False), me, 0)
    for shift in range(1, n_y):
        out = lax.dynamic_index_in_dim(chunks, (me + shift) % n_y, 0, False)
        moved = lax.ppermute(out, "ey", perm=[(i, (i + shift) % n_y) for i in range(n_y)])
        got = lax.dynamic_update_index_in_dim(got, moved, (me + n_y - shift) % n_y, 0)
    return got.reshape(send.shape)


def per_device(tokens, cotangent, expert_ids, combine, w_gate, w_up, w_down, tangent_gate):
    n_z = lax.axis_size("ez")
    n_y = lax.axis_size("ey")
    expert_count = n_z * n_y
    rows_dev, top_count = expert_ids.shape
    model_width = tokens.shape[1]
    capacity = rows_dev * top_count * 9 // (8 * expert_count)
    owners = jnp.arange(expert_count, dtype=jnp.int32)
    chosen = expert_ids[:, :, None] == owners[None, None, :]
    matches = chosen.astype(jnp.int32)
    named_count = jnp.sum(matches, axis=1)
    before = jnp.cumsum(named_count, axis=0) - named_count
    slot_pos = jnp.sum(before[:, None, :] * matches, axis=2)
    slots = expert_count * capacity
    in_slot = (named_count[:, :, None] > 0) & (
        before[:, :, None] == jnp.arange(capacity, dtype=jnp.int32)[None, None, :]
    )
    token_no = jnp.arange(rows_dev, dtype=jnp.float32)[:, None, None]
    src_of = jnp.sum(jnp.where(in_slot, token_no + 1.0, 0.0), axis=0) - 1.0
    weight_te = jnp.sum(jnp.where(chosen, combine[:, :, None], 0.0), axis=1)
    w_of = jnp.sum(jnp.where(in_slot, weight_te[:, :, None], 0.0), axis=0)
    table = jnp.stack((src_of,) + split3(w_of)).astype(jnp.bfloat16)
    extra = 16
    table = jnp.pad(table.reshape(-1), (0, extra * model_width - 4 * slots))
    packed = jnp.concatenate([tokens, table.reshape(extra, model_width)], axis=0)
    block = rows_dev + extra

    tok_g = lax.all_gather(packed, "ez", axis=0, tiled=True)
    cot_g = lax.all_gather(cotangent, "ez", axis=0, tiled=True)
    table_g = tok_g.reshape(n_z, block, model_width)[:, rows_dev:].reshape(n_z, -1)
    table_g = table_g[:, : 4 * slots].reshape(n_z, 4, expert_count, capacity)
    z_me = lax.axis_index("ez")
    mine = lax.dynamic_slice_in_dim(table_g, z_me * n_y, n_y, axis=2).astype(jnp.float32)
    mine = jnp.transpose(mine, (1, 2, 0, 3))
    src_tok = mine[0].astype(jnp.int32)
    src_w = (mine[1] + mine[2]) + mine[3]
    valid = src_tok >= 0
    z_of = jnp.arange(n_z, dtype=jnp.int32)[None, :, None]
    at_packed = jnp.where(valid, src_tok + z_of * block, -1).reshape(-1)
    at_cot = jnp.where(valid, src_tok + z_of * rows_dev, -1).reshape(-1)
    send_rows = select_rows(at_packed, tok_g).astype(jnp.bfloat16)

    rows_flat = lax.all_to_all(send_rows, "ey", split_axis=0, concat_axis=0, tiled=True)
    gate_e = w_gate[0]
    up_e = w_up[0]
    down_e = w_down[0]
    tangent_e = tangent_gate[0]
    send_scaled = (src_w.reshape(-1)[:, None] * select_rows(at_cot, cot_g)).astype(jnp.bfloat16)
    joined_e = jnp.concatenate([gate_e, up_e, tangent_e], axis=1)
    term, factor = forward_part(rows_flat, joined_e, down_e, (expert_count, capacity))
    returned = lax.all_to_all(term, ("ey", "ez"), split_axis=0, concat_axis=0, tiled=True)
    _, send_scaled = lax.optimization_barrier((rows_flat, send_scaled))
    scaled_flat = shift_along_y(send_scaled, n_y)
    coeff = backward_part(scaled_flat, down_e, factor)
    partial_hvp = lax.dot_general(
        rows_flat, coeff, (((0,), (0,)), ((), ())), preferred_element_type=jnp.float32
    )
    hvp_gate = lax.psum_scatter(partial_hvp, "dp", scatter_dimension=0, tiled=True)
    back_at = ((expert_ids % n_y) * n_z + expert_ids // n_y) * capacity + slot_pos
    at_slot = back_at[:, :, None] == jnp.arange(slots, dtype=jnp.int32)[None, None, :]
    spread = jnp.concatenate(
        [jnp.sum(jnp.where(at_slot, piece[:, :, None], 0.0), axis=1) for piece in split3(combine)], axis=0
    ).astype(jnp.bfloat16)
    by_piece = lax.dot_general(
        spread.reshape(3 * rows_dev, expert_count, capacity),
        returned,
        (((1, 2), (0, 1)), ((), ())),
        preferred_element_type=jnp.float32,
    ).reshape(3, rows_dev, model_width)
    output_tangent = (by_piece[0] + by_piece[1]) + by_piece[2]
    return (hvp_gate[None], output_tangent.astype(jnp.bfloat16))


def y_size(mesh):
    column = mesh.devices[0]
    try:
        return len({int(d.coords[1]) for d in column})
    except Exception:
        return 4


def solution(mesh):
    n_dp, n_expert = mesh.devices.shape
    n_y = y_size(mesh)
    mesh3 = Mesh(mesh.devices.reshape(n_dp, n_expert // n_y, n_y), ("dp", "ez", "ey"))
    rows = P(("dp", "ez", "ey"), None)
    weights = P(("ez", "ey"), None, None)
    placed = (rows, rows, rows, rows, weights, weights, weights, weights)
    return jax.shard_map(
        per_device,
        mesh=mesh3,
        in_specs=placed,
        out_specs=(P(("ez", "ey"), "dp", None), rows),
        check_vma=False,
    )
```

```python
import jax
import jax.numpy as jnp
import numpy as np
from jax import lax
from jax.sharding import Mesh
from jax.sharding import PartitionSpec as P


def silu_derivs(gate_act):
    squash = jax.nn.sigmoid(gate_act)
    first = squash * (1.0 + gate_act * (1.0 - squash))
    second = squash * (1.0 - squash) * (2.0 + gate_act * (1.0 - 2.0 * squash))
    return (first, second)


def forward_part(rows_flat, joined_e, down_e, blocks):
    hidden = down_e.shape[0]
    acts = jnp.dot(rows_flat, joined_e, preferred_element_type=jnp.float32)
    gate_act = acts[:, :hidden]
    up_act = acts[:, hidden : 2 * hidden]
    gate_dot = acts[:, 2 * hidden :]
    first, second = silu_derivs(gate_act)
    lifted = (first * gate_dot * up_act).astype(jnp.bfloat16)
    term = lax.dot_general(
        lifted.reshape(blocks + (lifted.shape[-1],)),
        down_e,
        (((2,), (0,)), ((), ())),
        preferred_element_type=jnp.float32,
    ).astype(jnp.bfloat16)
    return (term, up_act * second * gate_dot)


def backward_part(scaled_flat, down_e, factor):
    back_hidden = lax.dot_general(
        scaled_flat, down_e, (((1,), (1,)), ((), ())), preferred_element_type=jnp.float32
    )
    return (back_hidden * factor).astype(jnp.bfloat16)


def split3(value):
    hi = lax.reduce_precision(value, exponent_bits=8, mantissa_bits=7)
    rest = value - hi
    mid = lax.reduce_precision(rest, exponent_bits=8, mantissa_bits=7)
    return (hi, mid, rest - mid)


def select_rows(index, source):
    picks = (index[:, None] == jnp.arange(source.shape[0], dtype=jnp.int32)[None, :]).astype(source.dtype)
    return jnp.dot(picks, source, preferred_element_type=jnp.float32)


def shift_along_y(send, n_y):
    chunks = send.reshape(n_y, -1, send.shape[-1])
    me = lax.axis_index("ey")
    got = jnp.zeros_like(chunks)
    got = lax.dynamic_update_index_in_dim(got, chunks[0], me, 0)
    for shift in range(1, n_y):
        moved = lax.ppermute(chunks[shift], "ey", perm=[(i, (i + shift) % n_y) for i in range(n_y)])
        got = lax.dynamic_update_index_in_dim(got, moved, (me + n_y - shift) % n_y, 0)
    return got.reshape(send.shape)


def per_device(tokens, cotangent, expert_ids, combine, w_gate, w_up, w_down, tangent_gate):
    n_z = lax.axis_size("ez")
    n_y = lax.axis_size("ey")
    expert_count = n_z * n_y
    rows_dev, top_count = expert_ids.shape
    model_width = tokens.shape[1]
    capacity = rows_dev * top_count * 9 // (8 * expert_count)
    owners = jnp.arange(expert_count, dtype=jnp.int32)
    chosen = expert_ids[:, :, None] == owners[None, None, :]
    matches = chosen.astype(jnp.int32)
    named_count = jnp.sum(matches, axis=1)
    before = jnp.cumsum(named_count, axis=0) - named_count
    slot_pos = jnp.sum(before[:, None, :] * matches, axis=2)
    slots = expert_count * capacity
    in_slot = (named_count[:, :, None] > 0) & (
        before[:, :, None] == jnp.arange(capacity, dtype=jnp.int32)[None, None, :]
    )
    token_no = jnp.arange(rows_dev, dtype=jnp.float32)[:, None, None]
    src_of = jnp.sum(jnp.where(in_slot, token_no + 1.0, 0.0), axis=0) - 1.0
    weight_te = jnp.sum(jnp.where(chosen, combine[:, :, None], 0.0), axis=1)
    w_of = jnp.sum(jnp.where(in_slot, weight_te[:, :, None], 0.0), axis=0)
    table = jnp.stack((src_of,) + split3(w_of)).astype(jnp.bfloat16)
    extra = 16
    table = jnp.pad(table.reshape(-1), (0, extra * model_width - 4 * slots))
    packed = jnp.concatenate([tokens, table.reshape(extra, model_width)], axis=0)
    block = rows_dev + extra

    tok_g = lax.all_gather(packed, "ez", axis=0, tiled=True)
    cot_g = lax.all_gather(cotangent, "ez", axis=0, tiled=True)
    table_g = tok_g.reshape(n_z, block, model_width)[:, rows_dev:].reshape(n_z, -1)
    table_g = table_g[:, : 4 * slots].reshape(n_z, 4, expert_count, capacity)
    z_me = lax.axis_index("ez")
    mine = lax.dynamic_slice_in_dim(table_g, z_me * n_y, n_y, axis=2).astype(jnp.float32)
    mine = jnp.transpose(mine, (1, 2, 0, 3))
    src_tok = mine[0].astype(jnp.int32)
    src_w = (mine[1] + mine[2]) + mine[3]
    valid = src_tok >= 0
    z_of = jnp.arange(n_z, dtype=jnp.int32)[None, :, None]
    at_packed = jnp.where(valid, src_tok + z_of * block, -1).reshape(-1)
    at_cot = jnp.where(valid, src_tok + z_of * rows_dev, -1).reshape(-1)
    send_rows = select_rows(at_packed, tok_g).astype(jnp.bfloat16)

    rows_flat = lax.all_to_all(send_rows, "ey", split_axis=0, concat_axis=0, tiled=True)
    gate_e = w_gate[0]
    up_e = w_up[0]
    down_e = w_down[0]
    tangent_e = tangent_gate[0]
    rolled = (lax.axis_index("ey") + jnp.arange(n_y, dtype=jnp.int32)) % n_y
    at_rolled = jnp.take(at_cot.reshape(n_y, -1), rolled, axis=0).reshape(-1)
    w_rolled = jnp.take(src_w.reshape(n_y, -1), rolled, axis=0).reshape(-1)
    send_scaled = (w_rolled[:, None] * select_rows(at_rolled, cot_g)).astype(jnp.bfloat16)
    joined_e = jnp.concatenate([gate_e, up_e, tangent_e], axis=1)
    term, factor = forward_part(rows_flat, joined_e, down_e, (expert_count, capacity))
    returned = lax.all_to_all(term, ("ey", "ez"), split_axis=0, concat_axis=0, tiled=True)
    _, send_scaled = lax.optimization_barrier((rows_flat, send_scaled))
    scaled_flat = shift_along_y(send_scaled, n_y)
    coeff = backward_part(scaled_flat, down_e, factor)
    partial_hvp = lax.dot_general(
        rows_flat, coeff, (((0,), (0,)), ((), ())), preferred_element_type=jnp.float32
    )
    hvp_gate = lax.psum_scatter(partial_hvp, "dp", scatter_dimension=0, tiled=True)
    back_at = ((expert_ids % n_y) * n_z + expert_ids // n_y) * capacity + slot_pos
    at_slot = back_at[:, :, None] == jnp.arange(slots, dtype=jnp.int32)[None, None, :]
    spread = jnp.concatenate(
        [jnp.sum(jnp.where(at_slot, piece[:, :, None], 0.0), axis=1) for piece in split3(combine)], axis=0
    ).astype(jnp.bfloat16)
    by_piece = lax.dot_general(
        spread.reshape(3 * rows_dev, expert_count, capacity),
        returned,
        (((1, 2), (0, 1)), ((), ())),
        preferred_element_type=jnp.float32,
    ).reshape(3, rows_dev, model_width)
    output_tangent = (by_piece[0] + by_piece[1]) + by_piece[2]
    return (hvp_gate[None], output_tangent.astype(jnp.bfloat16))


def y_size(mesh):
    column = mesh.devices[0]
    try:
        return len({int(d.coords[1]) for d in column})
    except Exception:
        return 4


def solution(mesh):
    n_dp, n_expert = mesh.devices.shape
    n_y = y_size(mesh)
    mesh3 = Mesh(mesh.devices.reshape(n_dp, n_expert // n_y, n_y), ("dp", "ez", "ey"))
    rows = P(("dp", "ez", "ey"), None)
    weights = P(("ez", "ey"), None, None)
    placed = (rows, rows, rows, rows, weights, weights, weights, weights)
    return jax.shard_map(
        per_device,
        mesh=mesh3,
        in_specs=placed,
        out_specs=(P(("ez", "ey"), "dp", None), rows),
        check_vma=False,
    )
```

```python
import jax
import jax.numpy as jnp
import numpy as np
from jax import lax
from jax.sharding import Mesh
from jax.sharding import PartitionSpec as P


def silu_derivs(gate_act):
    squash = jax.nn.sigmoid(gate_act)
    first = squash * (1.0 + gate_act * (1.0 - squash))
    second = squash * (1.0 - squash) * (2.0 + gate_act * (1.0 - 2.0 * squash))
    return (first, second)


def forward_part(rows_flat, joined_e, down_e, blocks):
    hidden = down_e.shape[0]
    acts = jnp.dot(rows_flat, joined_e, preferred_element_type=jnp.float32)
    gate_act = acts[:, :hidden]
    up_act = acts[:, hidden : 2 * hidden]
    gate_dot = acts[:, 2 * hidden :]
    first, second = silu_derivs(gate_act)
    lifted = (first * gate_dot * up_act).astype(jnp.bfloat16)
    term = lax.dot_general(
        lifted.reshape(blocks + (lifted.shape[-1],)),
        down_e,
        (((2,), (0,)), ((), ())),
        preferred_element_type=jnp.float32,
    ).astype(jnp.bfloat16)
    return (term, up_act * second * gate_dot)


def backward_part(scaled_flat, down_e, factor):
    back_hidden = lax.dot_general(
        scaled_flat, down_e, (((1,), (1,)), ((), ())), preferred_element_type=jnp.float32
    )
    return (back_hidden * factor).astype(jnp.bfloat16)


def split3(value):
    hi = lax.reduce_precision(value, exponent_bits=8, mantissa_bits=7)
    rest = value - hi
    mid = lax.reduce_precision(rest, exponent_bits=8, mantissa_bits=7)
    return (hi, mid, rest - mid)


def select_rows(index, source):
    picks = (index[:, None] == jnp.arange(source.shape[0], dtype=jnp.int32)[None, :]).astype(source.dtype)
    return jnp.dot(picks, source, preferred_element_type=jnp.float32)


def shift_along_y(send, n_y):
    chunks = send.reshape(n_y, -1, send.shape[-1])
    me = lax.axis_index("ey")
    got = jnp.zeros_like(chunks)
    got = lax.dynamic_update_index_in_dim(got, chunks[0], me, 0)
    for shift in range(1, n_y):
        moved = lax.ppermute(chunks[shift], "ey", perm=[(i, (i + shift) % n_y) for i in range(n_y)])
        got = lax.dynamic_update_index_in_dim(got, moved, (me + n_y - shift) % n_y, 0)
    return got.reshape(send.shape)


def per_device(tokens, cotangent, expert_ids, combine, w_gate, w_up, w_down, tangent_gate):
    n_z = lax.axis_size("ez")
    n_y = lax.axis_size("ey")
    expert_count = n_z * n_y
    rows_dev, top_count = expert_ids.shape
    model_width = tokens.shape[1]
    capacity = rows_dev * top_count * 9 // (8 * expert_count)
    owners = jnp.arange(expert_count, dtype=jnp.int32)
    chosen = expert_ids[:, :, None] == owners[None, None, :]
    matches = chosen.astype(jnp.int32)
    named_count = jnp.sum(matches, axis=1)
    before = jnp.cumsum(named_count, axis=0) - named_count
    slot_pos = jnp.sum(before[:, None, :] * matches, axis=2)
    slots = expert_count * capacity
    in_slot = (named_count[:, :, None] > 0) & (
        before[:, :, None] == jnp.arange(capacity, dtype=jnp.int32)[None, None, :]
    )
    token_no = jnp.arange(rows_dev, dtype=jnp.float32)[:, None, None]
    src_of = jnp.sum(jnp.where(in_slot, token_no + 1.0, 0.0), axis=0) - 1.0
    weight_te = jnp.sum(jnp.where(chosen, combine[:, :, None], 0.0), axis=1)
    w_of = jnp.sum(jnp.where(in_slot, weight_te[:, :, None], 0.0), axis=0)
    table = jnp.stack((src_of,) + split3(w_of)).astype(jnp.bfloat16)
    extra = 16
    table = jnp.pad(table.reshape(-1), (0, extra * model_width - 4 * slots))
    packed = jnp.concatenate([tokens, table.reshape(extra, model_width)], axis=0)
    block = rows_dev + extra

    tok_g = lax.all_gather(packed, "ez", axis=0, tiled=True)
    cot_g = lax.all_gather(cotangent, "ez", axis=0, tiled=True)
    table_g = tok_g.reshape(n_z, block, model_width)[:, rows_dev:].reshape(n_z, -1)
    table_g = table_g[:, : 4 * slots].reshape(n_z, 4, expert_count, capacity)
    z_me = lax.axis_index("ez")
    mine = lax.dynamic_slice_in_dim(table_g, z_me * n_y, n_y, axis=2).astype(jnp.float32)
    mine = jnp.transpose(mine, (1, 2, 0, 3))
    src_tok = mine[0].astype(jnp.int32)
    src_w = (mine[1] + mine[2]) + mine[3]
    valid = src_tok >= 0
    z_of = jnp.arange(n_z, dtype=jnp.int32)[None, :, None]
    at_packed = jnp.where(valid, src_tok + z_of * block, -1).reshape(-1)
    at_cot = jnp.where(valid, src_tok + z_of * rows_dev, -1).reshape(-1)
    rolled = (lax.axis_index("ey") + jnp.arange(n_y, dtype=jnp.int32)) % n_y
    send_rows = select_rows(jnp.take(at_packed.reshape(n_y, -1), rolled, axis=0).reshape(-1), tok_g)
    send_rows = send_rows.astype(jnp.bfloat16)

    rows_flat = shift_along_y(send_rows, n_y)
    gate_e = w_gate[0]
    up_e = w_up[0]
    down_e = w_down[0]
    tangent_e = tangent_gate[0]
    at_rolled = jnp.take(at_cot.reshape(n_y, -1), rolled, axis=0).reshape(-1)
    w_rolled = jnp.take(src_w.reshape(n_y, -1), rolled, axis=0).reshape(-1)
    send_scaled = (w_rolled[:, None] * select_rows(at_rolled, cot_g)).astype(jnp.bfloat16)
    joined_e = jnp.concatenate([gate_e, up_e, tangent_e], axis=1)
    term, factor = forward_part(rows_flat, joined_e, down_e, (expert_count, capacity))
    returned = lax.all_to_all(term, ("ey", "ez"), split_axis=0, concat_axis=0, tiled=True)
    _, send_scaled = lax.optimization_barrier((rows_flat, send_scaled))
    scaled_flat = shift_along_y(send_scaled, n_y)
    coeff = backward_part(scaled_flat, down_e, factor)
    partial_hvp = lax.dot_general(
        rows_flat, coeff, (((0,), (0,)), ((), ())), preferred_element_type=jnp.float32
    )
    hvp_gate = lax.psum_scatter(partial_hvp, "dp", scatter_dimension=0, tiled=True)
    back_at = ((expert_ids % n_y) * n_z + expert_ids // n_y) * capacity + slot_pos
    at_slot = back_at[:, :, None] == jnp.arange(slots, dtype=jnp.int32)[None, None, :]
    spread = jnp.concatenate(
        [jnp.sum(jnp.where(at_slot, piece[:, :, None], 0.0), axis=1) for piece in split3(combine)], axis=0
    ).astype(jnp.bfloat16)
    by_piece = lax.dot_general(
        spread.reshape(3 * rows_dev, expert_count, capacity),
        returned,
        (((1, 2), (0, 1)), ((), ())),
        preferred_element_type=jnp.float32,
    ).reshape(3, rows_dev, model_width)
    output_tangent = (by_piece[0] + by_piece[1]) + by_piece[2]
    return (hvp_gate[None], output_tangent.astype(jnp.bfloat16))


def y_size(mesh):
    column = mesh.devices[0]
    try:
        return len({int(d.coords[1]) for d in column})
    except Exception:
        return 4


def solution(mesh):
    n_dp, n_expert = mesh.devices.shape
    n_y = y_size(mesh)
    mesh3 = Mesh(mesh.devices.reshape(n_dp, n_expert // n_y, n_y), ("dp", "ez", "ey"))
    rows = P(("dp", "ez", "ey"), None)
    weights = P(("ez", "ey"), None, None)
    placed = (rows, rows, rows, rows, weights, weights, weights, weights)
    return jax.shard_map(
        per_device,
        mesh=mesh3,
        in_specs=placed,
        out_specs=(P(("ez", "ey"), "dp", None), rows),
        check_vma=False,
    )
```

```python
import jax
import jax.numpy as jnp
import numpy as np
from jax import lax
from jax.sharding import Mesh
from jax.sharding import PartitionSpec as P


def silu_derivs(gate_act):
    squash = jax.nn.sigmoid(gate_act)
    first = squash * (1.0 + gate_act * (1.0 - squash))
    second = squash * (1.0 - squash) * (2.0 + gate_act * (1.0 - 2.0 * squash))
    return (first, second)


def forward_part(rows_flat, joined_e, down_e, blocks):
    hidden = down_e.shape[0]
    acts = jnp.dot(rows_flat, joined_e, preferred_element_type=jnp.float32)
    gate_act = acts[:, :hidden]
    up_act = acts[:, hidden : 2 * hidden]
    gate_dot = acts[:, 2 * hidden :]
    first, second = silu_derivs(gate_act)
    lifted = (first * gate_dot * up_act).astype(jnp.bfloat16)
    term = lax.dot_general(
        lifted.reshape(blocks + (lifted.shape[-1],)),
        down_e,
        (((2,), (0,)), ((), ())),
        preferred_element_type=jnp.float32,
    ).astype(jnp.bfloat16)
    return (term, up_act * second * gate_dot)


def backward_part(scaled_flat, down_e, factor):
    back_hidden = lax.dot_general(
        scaled_flat, down_e, (((1,), (1,)), ((), ())), preferred_element_type=jnp.float32
    )
    return (back_hidden * factor).astype(jnp.bfloat16)


def split3(value):
    hi = lax.reduce_precision(value, exponent_bits=8, mantissa_bits=7)
    rest = value - hi
    mid = lax.reduce_precision(rest, exponent_bits=8, mantissa_bits=7)
    return (hi, mid, rest - mid)


def select_rows(index, source):
    picks = (index[:, None] == jnp.arange(source.shape[0], dtype=jnp.int32)[None, :]).astype(source.dtype)
    return jnp.dot(picks, source, preferred_element_type=jnp.float32)


def shift_along_y(send, n_y):
    chunks = send.reshape(n_y, -1, send.shape[-1])
    me = lax.axis_index("ey")
    got = jnp.zeros_like(chunks)
    got = lax.dynamic_update_index_in_dim(got, lax.dynamic_index_in_dim(chunks, me, 0, False), me, 0)
    for shift in range(1, n_y):
        out = lax.dynamic_index_in_dim(chunks, (me + shift) % n_y, 0, False)
        moved = lax.ppermute(out, "ey", perm=[(i, (i + shift) % n_y) for i in range(n_y)])
        got = lax.dynamic_update_index_in_dim(got, moved, (me + n_y - shift) % n_y, 0)
    return got.reshape(send.shape)


def shift_along_z(recv, n_y, n_z):
    chunks = recv.reshape(n_y, n_z, -1, recv.shape[-1])
    me = lax.axis_index("ez")
    got = jnp.zeros_like(chunks)
    got = lax.dynamic_update_index_in_dim(got, chunks[:, 0], me, 1)
    for shift in range(1, n_z):
        moved = lax.ppermute(chunks[:, shift], "ez", perm=[(i, (i + shift) % n_z) for i in range(n_z)])
        got = lax.dynamic_update_index_in_dim(got, moved, (me + n_z - shift) % n_z, 1)
    return got.reshape(recv.shape)


def per_device(tokens, cotangent, expert_ids, combine, w_gate, w_up, w_down, tangent_gate):
    n_z = lax.axis_size("ez")
    n_y = lax.axis_size("ey")
    expert_count = n_z * n_y
    rows_dev, top_count = expert_ids.shape
    model_width = tokens.shape[1]
    capacity = rows_dev * top_count * 9 // (8 * expert_count)
    owners = jnp.arange(expert_count, dtype=jnp.int32)
    chosen = expert_ids[:, :, None] == owners[None, None, :]
    matches = chosen.astype(jnp.int32)
    named_count = jnp.sum(matches, axis=1)
    before = jnp.cumsum(named_count, axis=0) - named_count
    slot_pos = jnp.sum(before[:, None, :] * matches, axis=2)
    slots = expert_count * capacity
    in_slot = (named_count[:, :, None] > 0) & (
        before[:, :, None] == jnp.arange(capacity, dtype=jnp.int32)[None, None, :]
    )
    token_no = jnp.arange(rows_dev, dtype=jnp.float32)[:, None, None]
    src_of = jnp.sum(jnp.where(in_slot, token_no + 1.0, 0.0), axis=0) - 1.0
    weight_te = jnp.sum(jnp.where(chosen, combine[:, :, None], 0.0), axis=1)
    w_of = jnp.sum(jnp.where(in_slot, weight_te[:, :, None], 0.0), axis=0)
    z_here = lax.axis_index("ez")
    by_y = lambda t: t.reshape(n_z, n_y, capacity).transpose(1, 0, 2)
    z_roll = (z_here + jnp.arange(n_z, dtype=jnp.int32)) % n_z
    own_tok = jnp.take(by_y(src_of), z_roll, axis=1).reshape(-1).astype(jnp.int32)
    own_w = jnp.take(by_y(w_of), z_roll, axis=1).reshape(-1)
    send_c = (own_w[:, None] * select_rows(own_tok, cotangent)).astype(jnp.bfloat16)
    recv_c = lax.all_to_all(send_c, "ey", split_axis=0, concat_axis=0, tiled=True)
    table = jnp.stack((src_of,) + split3(w_of)).astype(jnp.bfloat16)
    extra = 16
    table = jnp.pad(table.reshape(-1), (0, extra * model_width - 4 * slots))
    packed = jnp.concatenate([tokens, table.reshape(extra, model_width)], axis=0)
    block = rows_dev + extra

    tok_g = lax.all_gather(packed, "ez", axis=0, tiled=True)
    table_g = tok_g.reshape(n_z, block, model_width)[:, rows_dev:].reshape(n_z, -1)
    table_g = table_g[:, : 4 * slots].reshape(n_z, 4, expert_count, capacity)
    z_me = lax.axis_index("ez")
    mine = lax.dynamic_slice_in_dim(table_g, z_me * n_y, n_y, axis=2).astype(jnp.float32)
    mine = jnp.transpose(mine, (1, 2, 0, 3))
    src_tok = mine[0].astype(jnp.int32)
    src_w = (mine[1] + mine[2]) + mine[3]
    valid = src_tok >= 0
    z_of = jnp.arange(n_z, dtype=jnp.int32)[None, :, None]
    at_packed = jnp.where(valid, src_tok + z_of * block, -1).reshape(-1)
    send_rows = select_rows(at_packed, tok_g).astype(jnp.bfloat16)

    rows_flat = lax.all_to_all(send_rows, "ey", split_axis=0, concat_axis=0, tiled=True)
    gate_e = w_gate[0]
    up_e = w_up[0]
    down_e = w_down[0]
    tangent_e = tangent_gate[0]
    joined_e = jnp.concatenate([gate_e, up_e, tangent_e], axis=1)
    term, factor = forward_part(rows_flat, joined_e, down_e, (expert_count, capacity))
    returned = lax.all_to_all(term, ("ey", "ez"), split_axis=0, concat_axis=0, tiled=True)
    scaled_flat = shift_along_z(recv_c, n_y, n_z)
    coeff = backward_part(scaled_flat, down_e, factor)
    partial_hvp = lax.dot_general(
        rows_flat, coeff, (((0,), (0,)), ((), ())), preferred_element_type=jnp.float32
    )
    hvp_gate = lax.psum_scatter(partial_hvp, "dp", scatter_dimension=0, tiled=True)
    back_at = ((expert_ids % n_y) * n_z + expert_ids // n_y) * capacity + slot_pos
    at_slot = back_at[:, :, None] == jnp.arange(slots, dtype=jnp.int32)[None, None, :]
    spread = jnp.concatenate(
        [jnp.sum(jnp.where(at_slot, piece[:, :, None], 0.0), axis=1) for piece in split3(combine)], axis=0
    ).astype(jnp.bfloat16)
    by_piece = lax.dot_general(
        spread.reshape(3 * rows_dev, expert_count, capacity),
        returned,
        (((1, 2), (0, 1)), ((), ())),
        preferred_element_type=jnp.float32,
    ).reshape(3, rows_dev, model_width)
    output_tangent = (by_piece[0] + by_piece[1]) + by_piece[2]
    return (hvp_gate[None], output_tangent.astype(jnp.bfloat16))


def y_size(mesh):
    column = mesh.devices[0]
    try:
        return len({int(d.coords[1]) for d in column})
    except Exception:
        return 4


def solution(mesh):
    n_dp, n_expert = mesh.devices.shape
    n_y = y_size(mesh)
    mesh3 = Mesh(mesh.devices.reshape(n_dp, n_expert // n_y, n_y), ("dp", "ez", "ey"))
    rows = P(("dp", "ez", "ey"), None)
    weights = P(("ez", "ey"), None, None)
    placed = (rows, rows, rows, rows, weights, weights, weights, weights)
    return jax.shard_map(
        per_device,
        mesh=mesh3,
        in_specs=placed,
        out_specs=(P(("ez", "ey"), "dp", None), rows),
        check_vma=False,
    )
```

```python
import jax
import jax.numpy as jnp
import numpy as np
from jax import lax
from jax.sharding import Mesh
from jax.sharding import PartitionSpec as P


def silu_derivs(gate_act):
    squash = jax.nn.sigmoid(gate_act)
    first = squash * (1.0 + gate_act * (1.0 - squash))
    second = squash * (1.0 - squash) * (2.0 + gate_act * (1.0 - 2.0 * squash))
    return (first, second)


def forward_part(rows_flat, joined_e, down_e, blocks):
    hidden = down_e.shape[0]
    acts = jnp.dot(rows_flat, joined_e, preferred_element_type=jnp.float32)
    gate_act = acts[:, :hidden]
    up_act = acts[:, hidden : 2 * hidden]
    gate_dot = acts[:, 2 * hidden :]
    first, second = silu_derivs(gate_act)
    lifted = (first * gate_dot * up_act).astype(jnp.bfloat16)
    term = lax.dot_general(
        lifted.reshape(blocks + (lifted.shape[-1],)),
        down_e,
        (((2,), (0,)), ((), ())),
        preferred_element_type=jnp.float32,
    ).astype(jnp.bfloat16)
    return (term, up_act * second * gate_dot)


def backward_part(scaled_flat, down_e, factor):
    back_hidden = lax.dot_general(
        scaled_flat, down_e, (((1,), (1,)), ((), ())), preferred_element_type=jnp.float32
    )
    return (back_hidden * factor).astype(jnp.bfloat16)


def split3(value):
    hi = lax.reduce_precision(value, exponent_bits=8, mantissa_bits=7)
    rest = value - hi
    mid = lax.reduce_precision(rest, exponent_bits=8, mantissa_bits=7)
    return (hi, mid, rest - mid)


def select_rows(index, source):
    picks = (index[:, None] == jnp.arange(source.shape[0], dtype=jnp.int32)[None, :]).astype(source.dtype)
    return jnp.dot(picks, source, preferred_element_type=jnp.float32)


def shift_along_y(send, n_y):
    chunks = send.reshape(n_y, -1, send.shape[-1])
    me = lax.axis_index("ey")
    arrived = [lax.dynamic_index_in_dim(chunks, me, 0, False)]
    for shift in range(1, n_y):
        out = lax.dynamic_index_in_dim(chunks, (me + shift) % n_y, 0, False)
        arrived.append(lax.ppermute(out, "ey", perm=[(i, (i + shift) % n_y) for i in range(n_y)]))
    got = [lax.select_n((me + n_y - p) % n_y, *arrived) for p in range(n_y)]
    return jnp.stack(got).reshape(send.shape)


def per_device(tokens, cotangent, expert_ids, combine, w_gate, w_up, w_down, tangent_gate):
    n_z = lax.axis_size("ez")
    n_y = lax.axis_size("ey")
    expert_count = n_z * n_y
    rows_dev, top_count = expert_ids.shape
    model_width = tokens.shape[1]
    capacity = rows_dev * top_count * 9 // (8 * expert_count)
    owners = jnp.arange(expert_count, dtype=jnp.int32)
    chosen = expert_ids[:, :, None] == owners[None, None, :]
    matches = chosen.astype(jnp.int32)
    named_count = jnp.sum(matches, axis=1)
    before = jnp.cumsum(named_count, axis=0) - named_count
    slot_pos = jnp.sum(before[:, None, :] * matches, axis=2)
    slots = expert_count * capacity
    in_slot = (named_count[:, :, None] > 0) & (
        before[:, :, None] == jnp.arange(capacity, dtype=jnp.int32)[None, None, :]
    )
    token_no = jnp.arange(rows_dev, dtype=jnp.float32)[:, None, None]
    src_of = jnp.sum(jnp.where(in_slot, token_no + 1.0, 0.0), axis=0) - 1.0
    weight_te = jnp.sum(jnp.where(chosen, combine[:, :, None], 0.0), axis=1)
    w_of = jnp.sum(jnp.where(in_slot, weight_te[:, :, None], 0.0), axis=0)
    table = jnp.stack((src_of,) + split3(w_of)).astype(jnp.bfloat16)
    extra = 16
    table = jnp.pad(table.reshape(-1), (0, extra * model_width - 4 * slots))
    packed = jnp.concatenate([tokens, table.reshape(extra, model_width)], axis=0)
    block = rows_dev + extra

    tok_g = lax.all_gather(packed, "ez", axis=0, tiled=True)
    cot_g = lax.all_gather(cotangent, "ez", axis=0, tiled=True)
    table_g = tok_g.reshape(n_z, block, model_width)[:, rows_dev:].reshape(n_z, -1)
    table_g = table_g[:, : 4 * slots].reshape(n_z, 4, expert_count, capacity)
    z_me = lax.axis_index("ez")
    mine = lax.dynamic_slice_in_dim(table_g, z_me * n_y, n_y, axis=2).astype(jnp.float32)
    mine = jnp.transpose(mine, (1, 2, 0, 3))
    src_tok = mine[0].astype(jnp.int32)
    src_w = (mine[1] + mine[2]) + mine[3]
    valid = src_tok >= 0
    z_of = jnp.arange(n_z, dtype=jnp.int32)[None, :, None]
    at_packed = jnp.where(valid, src_tok + z_of * block, -1).reshape(-1)
    at_cot = jnp.where(valid, src_tok + z_of * rows_dev, -1).reshape(-1)
    send_rows = select_rows(at_packed, tok_g).astype(jnp.bfloat16)

    rows_flat = lax.all_to_all(send_rows, "ey", split_axis=0, concat_axis=0, tiled=True)
    gate_e = w_gate[0]
    up_e = w_up[0]
    down_e = w_down[0]
    tangent_e = tangent_gate[0]
    send_scaled = (src_w.reshape(-1)[:, None] * select_rows(at_cot, cot_g)).astype(jnp.bfloat16)
    joined_e = jnp.concatenate([gate_e, up_e, tangent_e], axis=1)
    term, factor = forward_part(rows_flat, joined_e, down_e, (expert_count, capacity))
    returned = lax.all_to_all(term, ("ey", "ez"), split_axis=0, concat_axis=0, tiled=True)
    _, send_scaled = lax.optimization_barrier((rows_flat, send_scaled))
    scaled_flat = shift_along_y(send_scaled, n_y)
    coeff = backward_part(scaled_flat, down_e, factor)
    partial_hvp = lax.dot_general(
        rows_flat, coeff, (((0,), (0,)), ((), ())), preferred_element_type=jnp.float32
    )
    hvp_gate = lax.psum_scatter(partial_hvp, "dp", scatter_dimension=0, tiled=True)
    back_at = ((expert_ids % n_y) * n_z + expert_ids // n_y) * capacity + slot_pos
    at_slot = back_at[:, :, None] == jnp.arange(slots, dtype=jnp.int32)[None, None, :]
    spread = jnp.concatenate(
        [jnp.sum(jnp.where(at_slot, piece[:, :, None], 0.0), axis=1) for piece in split3(combine)], axis=0
    ).astype(jnp.bfloat16)
    by_piece = lax.dot_general(
        spread.reshape(3 * rows_dev, expert_count, capacity),
        returned,
        (((1, 2), (0, 1)), ((), ())),
        preferred_element_type=jnp.float32,
    ).reshape(3, rows_dev, model_width)
    output_tangent = (by_piece[0] + by_piece[1]) + by_piece[2]
    return (hvp_gate[None], output_tangent.astype(jnp.bfloat16))


def y_size(mesh):
    column = mesh.devices[0]
    try:
        return len({int(d.coords[1]) for d in column})
    except Exception:
        return 4


def solution(mesh):
    n_dp, n_expert = mesh.devices.shape
    n_y = y_size(mesh)
    mesh3 = Mesh(mesh.devices.reshape(n_dp, n_expert // n_y, n_y), ("dp", "ez", "ey"))
    rows = P(("dp", "ez", "ey"), None)
    weights = P(("ez", "ey"), None, None)
    placed = (rows, rows, rows, rows, weights, weights, weights, weights)
    return jax.shard_map(
        per_device,
        mesh=mesh3,
        in_specs=placed,
        out_specs=(P(("ez", "ey"), "dp", None), rows),
        check_vma=False,
    )
```
